32 devices in a mesh: grp: 2 (over x), date: 16 (over z, y, core).
Axes of the slice: x: 2, y: 2, z: 4, core: 2. Of those that a mesh axis runs over, the one named last changes fastest.
Arguments:
- slc: bfloat16 [16, 2, 128, 2048], P('date', None, 'grp'), parts along dimension 2, may hold values from -6 to 6
- pairs: int32 [64, 2], replicated, may hold values from 0 to 15, as said below
- inverse: bfloat16 [15, 64], replicated, may hold values from -6 to 6
Outputs:
- series: float32 [15, 32, 128], P(None, ('grp', 'date')), parts along dimension 1
The draws below stay inside these ranges and needn't reach their ends.
There are 2 independent parts, one for each index of `grp`. The reference program is written for one: setup_inputs(seed, part) draws one part's arguments, and reference() takes and returns one part's arrays. A program takes and returns all parts, laid end to end along the dimension named above; an argument that names none is the same for every part. Nothing has to cross between parts.
Inputs may be any that keep to these rules, and one draw needn't show every extreme that they name: pairs[p,0] < pairs[p,1] for every pair.
All inputs are finite; a program needn't handle non-finite values.
Results may differ from the reference program's by a relative error of at most 0.0003.
Values may be sent and summed in bfloat16 or wider, within the bound.
No kernel may reach another device: no remote copies, remote signals or barrier semaphores. Data moves between devices by JAX's collectives and lax.ppermute only.
A program may use at most 128 MiB of HBM per device.

```python
import jax
import jax.numpy as jnp
from jax import lax

COLS = 2048
LOOK_R = 4
LOOK_C = 16
NDATE = 16
STEPS = 15
PAIRS = 64
ROWS = 64


def draw_pairs(key, part):
    key_ref, key_gap = jax.random.split(jax.random.fold_in(key, 11))
    first = jax.random.randint(key_ref, (PAIRS,), 0, NDATE - 1)
    gap = jax.random.randint(key_gap, (PAIRS,), 1, NDATE // 2 + 1)
    second = jnp.minimum(first + gap, NDATE - 1)
    first = first.at[0].set(0)
    second = second.at[PAIRS - 1].set(NDATE - 1)
    return jnp.stack([first, second], axis=1).astype(jnp.int32)


def steps_of(stream_key, dims, cuts, low, top_value):
    loudness = 1.0
    for axis_at, blocks in cuts:
        draws = jax.random.uniform(jax.random.fold_in(jax.random.fold_in(stream_key, 6), axis_at), (blocks,), jnp.float32, low / len(cuts), top_value / len(cuts))
        loudness = loudness * jnp.repeat(jnp.exp(draws), dims[axis_at] // blocks).reshape((-1,) + (1,) * (len(dims) - 1 - axis_at))
    return loudness


def scatter_about(rng, shape, width, reach, shards=(), kind=jnp.bfloat16):
    drawn = width * jax.random.normal(rng, shape, jnp.float32)
    if shards:
        drawn = drawn * steps_of(rng, shape, shards, -0.22, 0.18)
    return jnp.clip(drawn, -reach, reach).astype(kind)


def setup_inputs(seed: int = 0, part: int = 0) -> dict:
    key_of = jax.random.split(jax.random.key(seed), 4)
    part_keys = jax.random.split(jax.random.fold_in(key_of[3], part), 4)
    return {
        "slc": scatter_about(part_keys[0], (NDATE, 2, ROWS, COLS), 1.0, 6.0, ((0, 16),)),
        "pairs": draw_pairs(jax.random.fold_in(key_of[3], 71), part),
        "inverse": scatter_about(key_of[2], (STEPS, PAIRS), (max(PAIRS // 64, 1)) ** -0.5, 6.0),
    }


def boxsum(values):
    count, rows, cols = values.shape
    return values.reshape(count, rows // LOOK_R, LOOK_R, cols // LOOK_C, LOOK_C).sum(axis=(2, 4))

def reference(slc, pairs, inverse):
    first = jnp.take(slc, pairs[:, 0], axis=0).astype(jnp.float32)
    second = jnp.take(slc, pairs[:, 1], axis=0).astype(jnp.float32)
    cross = first[:, 1] * second[:, 0] - first[:, 0] * second[:, 1]
    power_ref = first[:, 0] * first[:, 0] + first[:, 1] * first[:, 1]
    power_sec = second[:, 0] * second[:, 0] + second[:, 1] * second[:, 1]
    looked_cross = boxsum(cross)
    looked_ref = boxsum(power_ref)
    looked_sec = boxsum(power_sec)
    proxy = looked_cross / jnp.sqrt(looked_ref * looked_sec + 1e-06)
    return jnp.einsum('sp,pxy->sxy', inverse.astype(jnp.float32), proxy, precision=lax.Precision.HIGHEST)
```

```python
import functools

import jax
import jax.numpy as jnp
from jax import lax
from jax.experimental import pallas as pl
from jax.experimental.pallas import tpu as pltpu
from jax.sharding import PartitionSpec as P

LOOK_R = 4
LOOK_C = 16


def split3(x):
    hi = x.astype(jnp.bfloat16)
    rest = x - hi.astype(jnp.float32)
    mid = rest.astype(jnp.bfloat16)
    lo = (rest - mid.astype(jnp.float32)).astype(jnp.bfloat16)
    return hi, mid, lo


def dot3(parts, w, lhs_is_split):
    out = None
    for part in parts:
        if lhs_is_split:
            term = jnp.dot(part, w, preferred_element_type=jnp.float32)
        else:
            term = jnp.dot(w, part, preferred_element_type=jnp.float32)
        out = term if out is None else out + term
    return out


def kernel(n_date, n_pair, pairs_s, pairs_v, st_ref, inv_ref, out_ref, f_ref, rows_ref):
    cols = st_ref.shape[-1]
    looks = cols // LOOK_C

    def date_body(g, carry):
        acc = jnp.zeros((8, cols), jnp.float32)
        sub = lax.broadcasted_iota(jnp.int32, (8, cols), 0)
        for i in range(8):
            d = g * 8 + i
            re = st_ref[d, 0].astype(jnp.float32)
            im = st_ref[d, 1].astype(jnp.float32)
            f_ref[d, 0:LOOK_R, :] = re
            f_ref[d, LOOK_R:2 * LOOK_R, :] = im
            row = jnp.sum(re * re + im * im, axis=0, keepdims=True)
            acc = jnp.where(sub == i, jnp.broadcast_to(row, (8, cols)), acc)
        start = pl.multiple_of(n_pair + g * 8, 8)
        rows_ref[pl.ds(start, 8), :] = acc
        return carry

    lax.fori_loop(0, n_date // 8, date_body, 0)

    def pair_body(g, carry):
        acc = jnp.zeros((8, cols), jnp.float32)
        sub = lax.broadcasted_iota(jnp.int32, (8, cols), 0)
        for i in range(8):
            p = g * 8 + i
            a = pairs_s[2 * p]
            b = pairs_s[2 * p + 1]
            a0 = f_ref[a, 0:LOOK_R, :]
            a1 = f_ref[a, LOOK_R:2 * LOOK_R, :]
            b0 = f_ref[b, 0:LOOK_R, :]
            b1 = f_ref[b, LOOK_R:2 * LOOK_R, :]
            cross = a1 * b0 - a0 * b1
            row = jnp.sum(cross, axis=0, keepdims=True)
            acc = jnp.where(sub == i, jnp.broadcast_to(row, (8, cols)), acc)
        start = pl.multiple_of(g * 8, 8)
        rows_ref[pl.ds(start, 8), :] = acc
        return carry

    lax.fori_loop(0, n_pair // 8, pair_body, 0)

    c_idx = lax.broadcasted_iota(jnp.int32, (cols, looks), 0)
    j_idx = lax.broadcasted_iota(jnp.int32, (cols, looks), 1)
    window = ((c_idx >= j_idx * LOOK_C) & (c_idx < j_idx * LOOK_C + LOOK_C)).astype(jnp.bfloat16)
    looked = dot3(split3(rows_ref[...]), window, True)
    looked_cross = looked[0:n_pair]
    looked_pow = looked[n_pair:n_pair + n_date]

    date_idx = lax.broadcasted_iota(jnp.int32, (n_pair, n_date), 1)
    sel_a = (pairs_v[:, 0:1] == date_idx).astype(jnp.bfloat16)
    sel_b = (pairs_v[:, 1:2] == date_idx).astype(jnp.bfloat16)
    pow_parts = split3(looked_pow)
    looked_ref = dot3(pow_parts, sel_a, False)
    looked_sec = dot3(pow_parts, sel_b, False)

    proxy = looked_cross / jnp.sqrt(looked_ref * looked_sec + 1e-06)
    out_ref[...] = dot3(split3(proxy), inv_ref[...], False)


def per_device(slc, pairs, inverse):
    n_date = lax.axis_size("date")
    n_pair = pairs.shape[0]
    steps = inverse.shape[0]
    stripes = lax.all_to_all(slc, "date", split_axis=2, concat_axis=0, tiled=True)
    _, _, rows, cols = stripes.shape
    assert rows == LOOK_R and n_date % 8 == 0 and n_pair % 8 == 0
    looks = cols // LOOK_C
    out = pl.pallas_call(
        functools.partial(kernel, n_date, n_pair),
        out_shape=jax.ShapeDtypeStruct((steps, looks), jnp.float32),
        in_specs=[
            pl.BlockSpec(memory_space=pltpu.SMEM),
            pl.BlockSpec(memory_space=pltpu.VMEM),
            pl.BlockSpec(memory_space=pltpu.VMEM),
            pl.BlockSpec(memory_space=pltpu.VMEM),
        ],
        out_specs=pl.BlockSpec(memory_space=pltpu.VMEM),
        scratch_shapes=[
            pltpu.VMEM((n_date, 2 * LOOK_R, cols), jnp.float32),
            pltpu.VMEM((n_pair + n_date, cols), jnp.float32),
        ],
    )(pairs.reshape(-1), pairs, stripes, inverse)
    return out.reshape(steps, 1, looks)


def solution(mesh):
    in_specs = (P("date", None, "grp", None), P(), P())
    out_specs = P(None, ("grp", "date"), None)
    return jax.shard_map(
        per_device, mesh=mesh, in_specs=in_specs, out_specs=out_specs, check_vma=False
    )
```

```python
import functools

import jax
import jax.numpy as jnp
from jax import lax
from jax.experimental import pallas as pl
from jax.experimental.pallas import tpu as pltpu
from jax.sharding import PartitionSpec as P

LOOK_R = 4
LOOK_C = 16


def split3(x):
    hi = x.astype(jnp.bfloat16)
    rest = x - hi.astype(jnp.float32)
    mid = rest.astype(jnp.bfloat16)
    lo = (rest - mid.astype(jnp.float32)).astype(jnp.bfloat16)
    return hi, mid, lo


def dot3(parts, w, lhs_is_split):
    out = None
    for part in parts:
        if lhs_is_split:
            term = jnp.dot(part, w, preferred_element_type=jnp.float32)
        else:
            term = jnp.dot(w, part, preferred_element_type=jnp.float32)
        out = term if out is None else out + term
    return out


def kernel(n_date, n_pair, pairs_s, pairs_v, st_ref, inv_ref, out_ref, f_ref, rows_ref):
    cols = st_ref.shape[-1]
    looks = cols // LOOK_C

    def date_body(g, carry):
        acc = jnp.zeros((8, cols), jnp.float32)
        sub = lax.broadcasted_iota(jnp.int32, (8, cols), 0)
        for i in range(8):
            d = g * 8 + i
            re = st_ref[d, 0].astype(jnp.float32)
            im = st_ref[d, 1].astype(jnp.float32)
            f_ref[d, 0:LOOK_R, :] = re
            f_ref[d, LOOK_R:2 * LOOK_R, :] = im
            row = jnp.sum(re * re + im * im, axis=0, keepdims=True)
            acc = jnp.where(sub == i, jnp.broadcast_to(row, (8, cols)), acc)
        start = pl.multiple_of(n_pair + g * 8, 8)
        rows_ref[pl.ds(start, 8), :] = acc
        return carry

    lax.fori_loop(0, n_date // 8, date_body, 0)

    def pair_body(g, carry):
        acc = jnp.zeros((8, cols), jnp.float32)
        sub = lax.broadcasted_iota(jnp.int32, (8, cols), 0)
        for i in range(8):
            p = g * 8 + i
            a = pairs_s[p, 0]
            b = pairs_s[p, 1]
            a0 = f_ref[a, 0:LOOK_R, :]
            a1 = f_ref[a, LOOK_R:2 * LOOK_R, :]
            b0 = f_ref[b, 0:LOOK_R, :]
            b1 = f_ref[b, LOOK_R:2 * LOOK_R, :]
            cross = a1 * b0 - a0 * b1
            row = jnp.sum(cross, axis=0, keepdims=True)
            acc = jnp.where(sub == i, jnp.broadcast_to(row, (8, cols)), acc)
        start = pl.multiple_of(g * 8, 8)
        rows_ref[pl.ds(start, 8), :] = acc
        return carry

    lax.fori_loop(0, n_pair // 8, pair_body, 0)

    c_idx = lax.broadcasted_iota(jnp.int32, (cols, looks), 0)
    j_idx = lax.broadcasted_iota(jnp.int32, (cols, looks), 1)
    window = ((c_idx >= j_idx * LOOK_C) & (c_idx < j_idx * LOOK_C + LOOK_C)).astype(jnp.bfloat16)
    looked = dot3(split3(rows_ref[...]), window, True)
    looked_cross = looked[0:n_pair]
    looked_pow = looked[n_pair:n_pair + n_date]

    date_idx = lax.broadcasted_iota(jnp.int32, (n_pair, n_date), 1)
    sel_a = (pairs_v[:, 0:1] == date_idx).astype(jnp.bfloat16)
    sel_b = (pairs_v[:, 1:2] == date_idx).astype(jnp.bfloat16)
    pow_parts = split3(looked_pow)
    looked_ref = dot3(pow_parts, sel_a, False)
    looked_sec = dot3(pow_parts, sel_b, False)

    proxy = looked_cross / jnp.sqrt(looked_ref * looked_sec + 1e-06)
    series = dot3(split3(proxy), inv_ref[...], False)
    for s in range(series.shape[0]):
        out_ref[s] = series[s:s + 1, :]


def per_device(slc, pairs, inverse):
    n_date = lax.axis_size("date")
    n_pair = pairs.shape[0]
    steps = inverse.shape[0]
    stripes = lax.all_to_all(slc, "date", split_axis=2, concat_axis=0, tiled=True)
    _, _, rows, cols = stripes.shape
    assert rows == LOOK_R and n_date % 8 == 0 and n_pair % 8 == 0
    looks = cols // LOOK_C
    out = pl.pallas_call(
        functools.partial(kernel, n_date, n_pair),
        out_shape=jax.ShapeDtypeStruct((steps, 1, looks), jnp.float32),
        in_specs=[
            pl.BlockSpec(memory_space=pltpu.SMEM),
            pl.BlockSpec(memory_space=pltpu.VMEM),
            pl.BlockSpec(memory_space=pltpu.VMEM),
            pl.BlockSpec(memory_space=pltpu.VMEM),
        ],
        out_specs=pl.BlockSpec(memory_space=pltpu.VMEM),
        scratch_shapes=[
            pltpu.VMEM((n_date, 2 * LOOK_R, cols), jnp.float32),
            pltpu.VMEM((n_pair + n_date, cols), jnp.float32),
        ],
    )(pairs, pairs, stripes, inverse)
    return out


def solution(mesh):
    in_specs = (P("date", None, "grp", None), P(), P())
    out_specs = P(None, ("grp", "date"), None)
    return jax.shard_map(
        per_device, mesh=mesh, in_specs=in_specs, out_specs=out_specs, check_vma=False
    )
```

```python
import functools

import jax
import jax.numpy as jnp
from jax import lax
from jax.experimental import pallas as pl
from jax.experimental.pallas import tpu as pltpu
from jax.sharding import PartitionSpec as P

LOOK_R = 4
LOOK_C = 16


def split3(x):
    hi = x.astype(jnp.bfloat16)
    rest = x - hi.astype(jnp.float32)
    mid = rest.astype(jnp.bfloat16)
    lo = (rest - mid.astype(jnp.float32)).astype(jnp.bfloat16)
    return hi, mid, lo


def dot3(parts, w, lhs_is_split):
    out = None
    for part in parts:
        if lhs_is_split:
            term = jnp.dot(part, w, preferred_element_type=jnp.float32)
        else:
            term = jnp.dot(w, part, preferred_element_type=jnp.float32)
        out = term if out is None else out + term
    return out


def kernel(n_date, n_pair, pairs_s, pairs_v, st_ref, inv_ref, out_ref, f_ref, rows_ref):
    cols = st_ref.shape[-1]
    looks = cols // LOOK_C

    def date_body(g, carry):
        acc = jnp.zeros((8, cols), jnp.float32)
        sub = lax.broadcasted_iota(jnp.int32, (8, cols), 0)
        for i in range(8):
            d = g * 8 + i
            re = st_ref[d, 0].astype(jnp.float32)
            im = st_ref[d, 1].astype(jnp.float32)
            f_ref[d, 0:LOOK_R, :] = re
            f_ref[d, LOOK_R:2 * LOOK_R, :] = im
            row = jnp.sum(re * re + im * im, axis=0, keepdims=True)
            acc = jnp.where(sub == i, jnp.broadcast_to(row, (8, cols)), acc)
        start = pl.multiple_of(n_pair + g * 8, 8)
        rows_ref[pl.ds(start, 8), :] = acc
        return carry

    lax.fori_loop(0, n_date // 8, date_body, 0)

    def pair_body(g, carry):
        acc = jnp.zeros((8, cols), jnp.float32)
        sub = lax.broadcasted_iota(jnp.int32, (8, cols), 0)
        for i in range(8):
            p = g * 8 + i
            a = pairs_s[p, 0]
            b = pairs_s[p, 1]
            a0 = f_ref[a, 0:LOOK_R, :]
            a1 = f_ref[a, LOOK_R:2 * LOOK_R, :]
            b0 = f_ref[b, 0:LOOK_R, :]
            b1 = f_ref[b, LOOK_R:2 * LOOK_R, :]
            cross = a1 * b0 - a0 * b1
            row = jnp.sum(cross, axis=0, keepdims=True)
            acc = jnp.where(sub == i, jnp.broadcast_to(row, (8, cols)), acc)
        start = pl.multiple_of(g * 8, 8)
        rows_ref[pl.ds(start, 8), :] = acc
        return carry

    lax.fori_loop(0, n_pair // 8, pair_body, 0)

    c_idx = lax.broadcasted_iota(jnp.int32, (cols, looks), 0)
    j_idx = lax.broadcasted_iota(jnp.int32, (cols, looks), 1)
    window = ((c_idx >= j_idx * LOOK_C) & (c_idx < j_idx * LOOK_C + LOOK_C)).astype(jnp.bfloat16)
    looked = dot3(split3(rows_ref[...]), window, True)
    looked_cross = looked[0:n_pair]
    looked_pow = looked[n_pair:n_pair + n_date]

    date_idx = lax.broadcasted_iota(jnp.int32, (n_pair, n_date), 1)
    sel_a = (pairs_v[:, 0:1] == date_idx).astype(jnp.bfloat16)
    sel_b = (pairs_v[:, 1:2] == date_idx).astype(jnp.bfloat16)
    pow_parts = split3(looked_pow)
    looked_ref = dot3(pow_parts, sel_a, False)
    looked_sec = dot3(pow_parts, sel_b, False)

    proxy = looked_cross / jnp.sqrt(looked_ref * looked_sec + 1e-06)
    series = dot3(split3(proxy), inv_ref[...], False)
    for s in range(series.shape[0]):
        out_ref[s] = series[s:s + 1, :]


def per_device(slc, pairs, inverse):
    n_date = lax.axis_size("date")
    n_pair = pairs.shape[0]
    steps = inverse.shape[0]
    _, _, all_rows, cols = slc.shape
    rows = all_rows // n_date
    chunks = slc.reshape(2, n_date, rows, cols).transpose(1, 0, 2, 3)
    stripes = lax.all_to_all(chunks, "date", split_axis=0, concat_axis=0, tiled=True)
    assert rows == LOOK_R and n_date % 8 == 0 and n_pair % 8 == 0
    looks = cols // LOOK_C
    out = pl.pallas_call(
        functools.partial(kernel, n_date, n_pair),
        out_shape=jax.ShapeDtypeStruct((steps, 1, looks), jnp.float32),
        in_specs=[
            pl.BlockSpec(memory_space=pltpu.SMEM),
            pl.BlockSpec(memory_space=pltpu.VMEM),
            pl.BlockSpec(memory_space=pltpu.VMEM),
            pl.BlockSpec(memory_space=pltpu.VMEM),
        ],
        out_specs=pl.BlockSpec(memory_space=pltpu.VMEM),
        scratch_shapes=[
            pltpu.VMEM((n_date, 2 * LOOK_R, cols), jnp.float32),
            pltpu.VMEM((n_pair + n_date, cols), jnp.float32),
        ],
    )(pairs, pairs, stripes, inverse)
    return out


def solution(mesh):
    in_specs = (P("date", None, "grp", None), P(), P())
    out_specs = P(None, ("grp", "date"), None)
    return jax.shard_map(
        per_device, mesh=mesh, in_specs=in_specs, out_specs=out_specs, check_vma=False
    )
```

```python
import functools

import jax
import jax.numpy as jnp
from jax import lax
from jax.experimental import pallas as pl
from jax.experimental.pallas import tpu as pltpu
from jax.sharding import PartitionSpec as P

LOOK_R = 4
LOOK_C = 16


def split3(x):
    hi = x.astype(jnp.bfloat16)
    rest = x - hi.astype(jnp.float32)
    mid = rest.astype(jnp.bfloat16)
    lo = (rest - mid.astype(jnp.float32)).astype(jnp.bfloat16)
    return hi, mid, lo


def dot3(parts, w, lhs_is_split):
    out = None
    for part in parts:
        if lhs_is_split:
            term = jnp.dot(part, w, preferred_element_type=jnp.float32)
        else:
            term = jnp.dot(w, part, preferred_element_type=jnp.float32)
        out = term if out is None else out + term
    return out


def kernel(n_date, n_pair, *refs):
    pairs_s, pairs_v = refs[0], refs[1]
    st_refs = refs[2:2 + n_date]
    inv_ref, out_ref, f_ref, rows_ref = refs[2 + n_date:]
    cols = st_refs[0].shape[-1]
    looks = cols // LOOK_C

    sub = lax.broadcasted_iota(jnp.int32, (8, cols), 0)
    for g in range(n_date // 8):
        acc = jnp.zeros((8, cols), jnp.float32)
        for i in range(8):
            d = g * 8 + i
            re = st_refs[d][0].astype(jnp.float32)
            im = st_refs[d][1].astype(jnp.float32)
            f_ref[d, 0:LOOK_R, :] = re
            f_ref[d, LOOK_R:2 * LOOK_R, :] = im
            row = jnp.sum(re * re + im * im, axis=0, keepdims=True)
            acc = jnp.where(sub == i, jnp.broadcast_to(row, (8, cols)), acc)
        rows_ref[n_pair + g * 8:n_pair + g * 8 + 8, :] = acc

    def pair_body(g, carry):
        acc = jnp.zeros((8, cols), jnp.float32)
        sub = lax.broadcasted_iota(jnp.int32, (8, cols), 0)
        for i in range(8):
            p = g * 8 + i
            a = pairs_s[p, 0]
            b = pairs_s[p, 1]
            a0 = f_ref[a, 0:LOOK_R, :]
            a1 = f_ref[a, LOOK_R:2 * LOOK_R, :]
            b0 = f_ref[b, 0:LOOK_R, :]
            b1 = f_ref[b, LOOK_R:2 * LOOK_R, :]
            cross = a1 * b0 - a0 * b1
            row = jnp.sum(cross, axis=0, keepdims=True)
            acc = jnp.where(sub == i, jnp.broadcast_to(row, (8, cols)), acc)
        start = pl.multiple_of(g * 8, 8)
        rows_ref[pl.ds(start, 8), :] = acc
        return carry

    lax.fori_loop(0, n_pair // 8, pair_body, 0)

    c_idx = lax.broadcasted_iota(jnp.int32, (cols, looks), 0)
    j_idx = lax.broadcasted_iota(jnp.int32, (cols, looks), 1)
    window = ((c_idx >= j_idx * LOOK_C) & (c_idx < j_idx * LOOK_C + LOOK_C)).astype(jnp.bfloat16)
    looked = dot3(split3(rows_ref[...]), window, True)
    looked_cross = looked[0:n_pair]
    looked_pow = looked[n_pair:n_pair + n_date]

    date_idx = lax.broadcasted_iota(jnp.int32, (n_pair, n_date), 1)
    sel_a = (pairs_v[:, 0:1] == date_idx).astype(jnp.bfloat16)
    sel_b = (pairs_v[:, 1:2] == date_idx).astype(jnp.bfloat16)
    pow_parts = split3(looked_pow)
    looked_ref = dot3(pow_parts, sel_a, False)
    looked_sec = dot3(pow_parts, sel_b, False)

    proxy = looked_cross / jnp.sqrt(looked_ref * looked_sec + 1e-06)
    series = dot3(split3(proxy), inv_ref[...], False)
    for s in range(series.shape[0]):
        out_ref[s] = series[s:s + 1, :]


def per_device(slc, pairs, inverse):
    n_date = lax.axis_size("date")
    n_pair = pairs.shape[0]
    steps = inverse.shape[0]
    me = lax.axis_index("date")
    _, _, all_rows, cols = slc.shape
    rows = all_rows // n_date
    assert rows == LOOK_R and n_date % 8 == 0 and n_pair % 8 == 0
    rolled = jnp.roll(slc[0], -me * rows, axis=1).reshape(2, n_date, rows, cols).transpose(1, 0, 2, 3)
    pieces = [rolled[0]]
    for k in range(1, n_date):
        perm = [(i, (i + k) % n_date) for i in range(n_date)]
        pieces.append(lax.ppermute(rolled[k], "date", perm))
    slots = (me - pairs + n_date) % n_date
    looks = cols // LOOK_C
    out = pl.pallas_call(
        functools.partial(kernel, n_date, n_pair),
        out_shape=jax.ShapeDtypeStruct((steps, 1, looks), jnp.float32),
        in_specs=[pl.BlockSpec(memory_space=pltpu.SMEM)]
        + [pl.BlockSpec(memory_space=pltpu.VMEM)] * (n_date + 2),
        out_specs=pl.BlockSpec(memory_space=pltpu.VMEM),
        scratch_shapes=[
            pltpu.VMEM((n_date, 2 * LOOK_R, cols), jnp.float32),
            pltpu.VMEM((n_pair + n_date, cols), jnp.float32),
        ],
    )(slots, slots, *pieces, inverse)
    return out


def solution(mesh):
    in_specs = (P("date", None, "grp", None), P(), P())
    out_specs = P(None, ("grp", "date"), None)
    return jax.shard_map(
        per_device, mesh=mesh, in_specs=in_specs, out_specs=out_specs, check_vma=False
    )
```

```python
import functools

import jax
import jax.numpy as jnp
from jax import lax
from jax.experimental import pallas as pl
from jax.experimental.pallas import tpu as pltpu
from jax.sharding import PartitionSpec as P

LOOK_R = 4
LOOK_C = 16


def split3(x):
    hi = x.astype(jnp.bfloat16)
    rest = x - hi.astype(jnp.float32)
    mid = rest.astype(jnp.bfloat16)
    lo = (rest - mid.astype(jnp.float32)).astype(jnp.bfloat16)
    return hi, mid, lo


def dot3(parts, w, lhs_is_split):
    out = None
    for part in parts:
        if lhs_is_split:
            term = jnp.dot(part, w, preferred_element_type=jnp.float32)
        else:
            term = jnp.dot(w, part, preferred_element_type=jnp.float32)
        out = term if out is None else out + term
    return out


def kernel(n_date, n_pair, pairs_s, pairs_v, st_ref, inv_ref, out_ref, f_ref, rows_ref):
    cols = st_ref.shape[-1]
    looks = cols // LOOK_C

    def date_body(g, carry):
        acc = jnp.zeros((8, cols), jnp.float32)
        sub = lax.broadcasted_iota(jnp.int32, (8, cols), 0)
        for i in range(8):
            d = g * 8 + i
            row = None
            for r in range(LOOK_R):
                v = st_ref[d * LOOK_R + r].astype(jnp.float32)
                re = v[0:1]
                im = v[1:2]
                f_ref[d, r:r + 1, :] = re
                f_ref[d, LOOK_R + r:LOOK_R + r + 1, :] = im
                pw = re * re + im * im
                row = pw if row is None else row + pw
            acc = jnp.where(sub == i, jnp.broadcast_to(row, (8, cols)), acc)
        start = pl.multiple_of(n_pair + g * 8, 8)
        rows_ref[pl.ds(start, 8), :] = acc
        return carry

    lax.fori_loop(0, n_date // 8, date_body, 0)

    def pair_body(g, carry):
        acc = jnp.zeros((8, cols), jnp.float32)
        sub = lax.broadcasted_iota(jnp.int32, (8, cols), 0)
        for i in range(8):
            p = g * 8 + i
            a = pairs_s[p, 0]
            b = pairs_s[p, 1]
            a0 = f_ref[a, 0:LOOK_R, :]
            a1 = f_ref[a, LOOK_R:2 * LOOK_R, :]
            b0 = f_ref[b, 0:LOOK_R, :]
            b1 = f_ref[b, LOOK_R:2 * LOOK_R, :]
            cross = a1 * b0 - a0 * b1
            row = jnp.sum(cross, axis=0, keepdims=True)
            acc = jnp.where(sub == i, jnp.broadcast_to(row, (8, cols)), acc)
        start = pl.multiple_of(g * 8, 8)
        rows_ref[pl.ds(start, 8), :] = acc
        return carry

    lax.fori_loop(0, n_pair // 8, pair_body, 0)

    c_idx = lax.broadcasted_iota(jnp.int32, (cols, looks), 0)
    j_idx = lax.broadcasted_iota(jnp.int32, (cols, looks), 1)
    window = ((c_idx >= j_idx * LOOK_C) & (c_idx < j_idx * LOOK_C + LOOK_C)).astype(jnp.bfloat16)
    looked = dot3(split3(rows_ref[...]), window, True)
    looked_cross = looked[0:n_pair]
    looked_pow = looked[n_pair:n_pair + n_date]

    date_idx = lax.broadcasted_iota(jnp.int32, (n_pair, n_date), 1)
    sel_a = (pairs_v[:, 0:1] == date_idx).astype(jnp.bfloat16)
    sel_b = (pairs_v[:, 1:2] == date_idx).astype(jnp.bfloat16)
    pow_parts = split3(looked_pow)
    looked_ref = dot3(pow_parts, sel_a, False)
    looked_sec = dot3(pow_parts, sel_b, False)

    proxy = looked_cross / jnp.sqrt(looked_ref * looked_sec + 1e-06)
    series = dot3(split3(proxy), inv_ref[...], False)
    for s in range(series.shape[0]):
        out_ref[s] = series[s:s + 1, :]


def per_device(slc, pairs, inverse):
    n_date = lax.axis_size("date")
    n_pair = pairs.shape[0]
    steps = inverse.shape[0]
    _, _, all_rows, cols = slc.shape
    rows = all_rows // n_date
    got = lax.all_to_all(slc, "date", split_axis=2, concat_axis=2, tiled=True)
    stripes = got[0].transpose(1, 0, 2)
    assert rows == LOOK_R and n_date % 8 == 0 and n_pair % 8 == 0
    looks = cols // LOOK_C
    out = pl.pallas_call(
        functools.partial(kernel, n_date, n_pair),
        out_shape=jax.ShapeDtypeStruct((steps, 1, looks), jnp.float32),
        in_specs=[
            pl.BlockSpec(memory_space=pltpu.SMEM),
            pl.BlockSpec(memory_space=pltpu.VMEM),
            pl.BlockSpec(memory_space=pltpu.VMEM),
            pl.BlockSpec(memory_space=pltpu.VMEM),
        ],
        out_specs=pl.BlockSpec(memory_space=pltpu.VMEM),
        scratch_shapes=[
            pltpu.VMEM((n_date, 2 * LOOK_R, cols), jnp.float32),
            pltpu.VMEM((n_pair + n_date, cols), jnp.float32),
        ],
    )(pairs, pairs, stripes, inverse)
    return out


def solution(mesh):
    in_specs = (P("date", None, "grp", None), P(), P())
    out_specs = P(None, ("grp", "date"), None)
    return jax.shard_map(
        per_device, mesh=mesh, in_specs=in_specs, out_specs=out_specs, check_vma=False
    )
```

```python
import functools

import jax
import jax.numpy as jnp
from jax import lax
from jax.experimental import pallas as pl
from jax.experimental.pallas import tpu as pltpu
from jax.sharding import PartitionSpec as P

LOOK_R = 4
LOOK_C = 16


def split3(x):
    hi = x.astype(jnp.bfloat16)
    rest = x - hi.astype(jnp.float32)
    mid = rest.astype(jnp.bfloat16)
    lo = (rest - mid.astype(jnp.float32)).astype(jnp.bfloat16)
    return hi, mid, lo


def dot3(parts, w, lhs_is_split):
    out = None
    for part in parts:
        if lhs_is_split:
            term = jnp.dot(part, w, preferred_element_type=jnp.float32)
        else:
            term = jnp.dot(w, part, preferred_element_type=jnp.float32)
        out = term if out is None else out + term
    return out


def kernel(n_date, n_pair, pairs_s, pairs_v, st_ref, inv_ref, out_ref, f_ref, g_ref, rows_ref):
    cols = st_ref.shape[-1]
    looks = cols // LOOK_C

    def date_body(g, carry):
        acc = jnp.zeros((8, cols), jnp.float32)
        sub = lax.broadcasted_iota(jnp.int32, (8, cols), 0)
        for i in range(8):
            d = g * 8 + i
            row = None
            for r in range(LOOK_R):
                v = st_ref[d * LOOK_R + r].astype(jnp.float32)
                re = v[0:1]
                im = v[1:2]
                f_ref[d, r:r + 1, :] = re
                f_ref[d, LOOK_R + r:LOOK_R + r + 1, :] = im
                pw = re * re + im * im
                row = pw if row is None else row + pw
            acc = jnp.where(sub == i, jnp.broadcast_to(row, (8, cols)), acc)
        start = pl.multiple_of(n_pair + g * 8, 8)
        rows_ref[pl.ds(start, 8), :] = acc
        return carry

    lax.fori_loop(0, n_date // 8, date_body, 0)

    sub = lax.broadcasted_iota(jnp.int32, (2 * LOOK_R, cols), 0)
    sign = jnp.where(sub < LOOK_R, -1.0, 1.0).astype(jnp.float32)

    def swap_body(d, carry):
        g_ref[d] = pltpu.roll(f_ref[d], LOOK_R, 0) * sign
        return carry

    lax.fori_loop(0, n_date, swap_body, 0)

    masks = {h: (sub & h) == 0 for h in (4, 2, 1)}

    def combine(x, y, h):
        m = masks[h]
        w = jnp.where(m, y, x)
        if h == 4:
            moved = pltpu.roll(w, 4, 0)
        else:
            moved = jnp.where(m, pltpu.roll(w, 8 - h, 0), pltpu.roll(w, h, 0))
        return jnp.where(m, x, y) + moved

    def pair_body(g, carry):
        level = []
        for i in (0, 4, 2, 6, 1, 5, 3, 7):
            p = g * 8 + i
            level.append(f_ref[pairs_s[p, 0]] * g_ref[pairs_s[p, 1]])
        for h in (4, 2, 1):
            level = [combine(level[2 * j], level[2 * j + 1], h) for j in range(len(level) // 2)]
        start = pl.multiple_of(g * 8, 8)
        rows_ref[pl.ds(start, 8), :] = level[0]
        return carry

    lax.fori_loop(0, n_pair // 8, pair_body, 0)

    c_idx = lax.broadcasted_iota(jnp.int32, (cols, looks), 0)
    j_idx = lax.broadcasted_iota(jnp.int32, (cols, looks), 1)
    window = ((c_idx >= j_idx * LOOK_C) & (c_idx < j_idx * LOOK_C + LOOK_C)).astype(jnp.bfloat16)
    looked = dot3(split3(rows_ref[...]), window, True)
    looked_cross = looked[0:n_pair]
    looked_pow = looked[n_pair:n_pair + n_date]

    date_idx = lax.broadcasted_iota(jnp.int32, (n_pair, n_date), 1)
    sel_a = (pairs_v[:, 0:1] == date_idx).astype(jnp.bfloat16)
    sel_b = (pairs_v[:, 1:2] == date_idx).astype(jnp.bfloat16)
    pow_parts = split3(looked_pow)
    looked_ref = dot3(pow_parts, sel_a, False)
    looked_sec = dot3(pow_parts, sel_b, False)

    proxy = looked_cross / jnp.sqrt(looked_ref * looked_sec + 1e-06)
    series = dot3(split3(proxy), inv_ref[...], False)
    for s in range(series.shape[0]):
        out_ref[s] = series[s:s + 1, :]


def per_device(slc, pairs, inverse):
    n_date = lax.axis_size("date")
    n_pair = pairs.shape[0]
    steps = inverse.shape[0]
    _, _, all_rows, cols = slc.shape
    rows = all_rows // n_date
    got = lax.all_to_all(slc, "date", split_axis=2, concat_axis=2, tiled=True)
    stripes = got[0].transpose(1, 0, 2)
    assert rows == LOOK_R and n_date % 8 == 0 and n_pair % 8 == 0
    looks = cols // LOOK_C
    out = pl.pallas_call(
        functools.partial(kernel, n_date, n_pair),
        out_shape=jax.ShapeDtypeStruct((steps, 1, looks), jnp.float32),
        in_specs=[
            pl.BlockSpec(memory_space=pltpu.SMEM),
            pl.BlockSpec(memory_space=pltpu.VMEM),
            pl.BlockSpec(memory_space=pltpu.VMEM),
            pl.BlockSpec(memory_space=pltpu.VMEM),
        ],
        out_specs=pl.BlockSpec(memory_space=pltpu.VMEM),
        scratch_shapes=[
            pltpu.VMEM((n_date, 2 * LOOK_R, cols), jnp.float32),
            pltpu.VMEM((n_date, 2 * LOOK_R, cols), jnp.float32),
            pltpu.VMEM((n_pair + n_date, cols), jnp.float32),
        ],
    )(pairs, pairs, stripes, inverse)
    return out


def solution(mesh):
    in_specs = (P("date", None, "grp", None), P(), P())
    out_specs = P(None, ("grp", "date"), None)
    return jax.shard_map(
        per_device, mesh=mesh, in_specs=in_specs, out_specs=out_specs, check_vma=False
    )
```

```python
import functools

import jax
import jax.numpy as jnp
from jax import lax
from jax.experimental import pallas as pl
from jax.experimental.pallas import tpu as pltpu
from jax.sharding import PartitionSpec as P

LOOK_R = 4
LOOK_C = 16


def split3(x):
    hi = x.astype(jnp.bfloat16)
    rest = x - hi.astype(jnp.float32)
    mid = rest.astype(jnp.bfloat16)
    lo = (rest - mid.astype(jnp.float32)).astype(jnp.bfloat16)
    return hi, mid, lo


def dot3(parts, w, lhs_is_split):
    out = None
    for part in parts:
        if lhs_is_split:
            term = jnp.dot(part, w, preferred_element_type=jnp.float32)
        else:
            term = jnp.dot(w, part, preferred_element_type=jnp.float32)
        out = term if out is None else out + term
    return out


def kernel(n_date, n_pair, pairs_s, pairs_v, st_ref, inv_ref, out_ref, f_ref, g_ref, rows_ref):
    cols = st_ref.shape[-1]
    looks = cols // LOOK_C

    def date_body(g, carry):
        acc = jnp.zeros((8, cols), jnp.float32)
        sub = lax.broadcasted_iota(jnp.int32, (8, cols), 0)
        for i in range(8):
            d = g * 8 + i
            re = st_ref[d, 0].astype(jnp.float32)
            im = st_ref[d, 1].astype(jnp.float32)
            f_ref[d, 0:LOOK_R, :] = re
            f_ref[d, LOOK_R:2 * LOOK_R, :] = im
            row = jnp.sum(re * re + im * im, axis=0, keepdims=True)
            acc = jnp.where(sub == i, jnp.broadcast_to(row, (8, cols)), acc)
        start = pl.multiple_of(n_pair + g * 8, 8)
        rows_ref[pl.ds(start, 8), :] = acc
        return carry

    lax.fori_loop(0, n_date // 8, date_body, 0)

    sub = lax.broadcasted_iota(jnp.int32, (2 * LOOK_R, cols), 0)
    sign = jnp.where(sub < LOOK_R, -1.0, 1.0).astype(jnp.float32)

    def swap_body(d, carry):
        g_ref[d] = pltpu.roll(f_ref[d], LOOK_R, 0) * sign
        return carry

    lax.fori_loop(0, n_date, swap_body, 0)

    masks = {h: (sub & h) == 0 for h in (4, 2, 1)}

    def combine(x, y, h):
        m = masks[h]
        w = jnp.where(m, y, x)
        if h == 4:
            moved = pltpu.roll(w, 4, 0)
        else:
            moved = jnp.where(m, pltpu.roll(w, 8 - h, 0), pltpu.roll(w, h, 0))
        return jnp.where(m, x, y) + moved

    def pair_body(g, carry):
        level = []
        for i in (0, 4, 2, 6, 1, 5, 3, 7):
            p = g * 8 + i
            level.append(f_ref[pairs_s[p, 0]] * g_ref[pairs_s[p, 1]])
        for h in (4, 2, 1):
            level = [combine(level[2 * j], level[2 * j + 1], h) for j in range(len(level) // 2)]
        start = pl.multiple_of(g * 8, 8)
        rows_ref[pl.ds(start, 8), :] = level[0]
        return carry

    lax.fori_loop(0, n_pair // 8, pair_body, 0)

    c_idx = lax.broadcasted_iota(jnp.int32, (cols, looks), 0)
    j_idx = lax.broadcasted_iota(jnp.int32, (cols, looks), 1)
    window = ((c_idx >= j_idx * LOOK_C) & (c_idx < j_idx * LOOK_C + LOOK_C)).astype(jnp.bfloat16)
    looked = dot3(split3(rows_ref[...]), window, True)
    looked_cross = looked[0:n_pair]
    looked_pow = looked[n_pair:n_pair + n_date]

    date_idx = lax.broadcasted_iota(jnp.int32, (n_pair, n_date), 1)
    sel_a = (pairs_v[:, 0:1] == date_idx).astype(jnp.bfloat16)
    sel_b = (pairs_v[:, 1:2] == date_idx).astype(jnp.bfloat16)
    pow_parts = split3(looked_pow)
    looked_ref = dot3(pow_parts, sel_a, False)
    looked_sec = dot3(pow_parts, sel_b, False)

    proxy = looked_cross / jnp.sqrt(looked_ref * looked_sec + 1e-06)
    series = dot3(split3(proxy), inv_ref[...], False)
    for s in range(series.shape[0]):
        out_ref[s] = series[s:s + 1, :]


def regroup_kernel(in_ref, out_ref):
    for c in range(out_ref.shape[0]):
        for k in range(2):
            out_ref[c, k] = in_ref[k, c * LOOK_R:(c + 1) * LOOK_R, :]


def per_device(slc, pairs, inverse):
    n_date = lax.axis_size("date")
    n_pair = pairs.shape[0]
    steps = inverse.shape[0]
    _, _, all_rows, cols = slc.shape
    rows = all_rows // n_date
    chunks = pl.pallas_call(
        regroup_kernel,
        out_shape=jax.ShapeDtypeStruct((n_date, 2, rows, cols), slc.dtype),
        in_specs=[pl.BlockSpec(memory_space=pltpu.VMEM)],
        out_specs=pl.BlockSpec(memory_space=pltpu.VMEM),
    )(slc[0])
    stripes = lax.all_to_all(chunks, "date", split_axis=0, concat_axis=0, tiled=True)
    assert rows == LOOK_R and n_date % 8 == 0 and n_pair % 8 == 0
    looks = cols // LOOK_C
    out = pl.pallas_call(
        functools.partial(kernel, n_date, n_pair),
        out_shape=jax.ShapeDtypeStruct((steps, 1, looks), jnp.float32),
        in_specs=[
            pl.BlockSpec(memory_space=pltpu.SMEM),
            pl.BlockSpec(memory_space=pltpu.VMEM),
            pl.BlockSpec(memory_space=pltpu.VMEM),
            pl.BlockSpec(memory_space=pltpu.VMEM),
        ],
        out_specs=pl.BlockSpec(memory_space=pltpu.VMEM),
        scratch_shapes=[
            pltpu.VMEM((n_date, 2 * LOOK_R, cols), jnp.float32),
            pltpu.VMEM((n_date, 2 * LOOK_R, cols), jnp.float32),
            pltpu.VMEM((n_pair + n_date, cols), jnp.float32),
        ],
    )(pairs, pairs, stripes, inverse)
    return out


def solution(mesh):
    in_specs = (P("date", None, "grp", None), P(), P())
    out_specs = P(None, ("grp", "date"), None)
    return jax.shard_map(
        per_device, mesh=mesh, in_specs=in_specs, out_specs=out_specs, check_vma=False
    )
```

```python
import functools

import jax
import jax.numpy as jnp
from jax import lax
from jax.experimental import pallas as pl
from jax.experimental.pallas import tpu as pltpu
from jax.sharding import PartitionSpec as P

LOOK_R = 4
LOOK_C = 16


def split3(x):
    hi = x.astype(jnp.bfloat16)
    rest = x - hi.astype(jnp.float32)
    mid = rest.astype(jnp.bfloat16)
    lo = (rest - mid.astype(jnp.float32)).astype(jnp.bfloat16)
    return hi, mid, lo


def dot3(parts, w, lhs_is_split):
    out = None
    for part in parts:
        if lhs_is_split:
            term = jnp.dot(part, w, preferred_element_type=jnp.float32)
        else:
            term = jnp.dot(w, part, preferred_element_type=jnp.float32)
        out = term if out is None else out + term
    return out


def kernel(n_date, n_pair, pairs_s, pairs_v, st_any, inv_ref, out_ref, f_ref, g_ref, rows_ref, st_ref):
    pltpu.sync_copy(st_any, st_ref)
    cols = st_ref.shape[-1]
    looks = cols // LOOK_C

    def date_body(g, carry):
        acc = jnp.zeros((8, cols), jnp.float32)
        sub = lax.broadcasted_iota(jnp.int32, (8, cols), 0)
        for i in range(8):
            d = g * 8 + i
            re = st_ref[d, 0].astype(jnp.float32)
            im = st_ref[d, 1].astype(jnp.float32)
            f_ref[d, 0:LOOK_R, :] = re
            f_ref[d, LOOK_R:2 * LOOK_R, :] = im
            row = jnp.sum(re * re + im * im, axis=0, keepdims=True)
            acc = jnp.where(sub == i, jnp.broadcast_to(row, (8, cols)), acc)
        start = pl.multiple_of(n_pair + g * 8, 8)
        rows_ref[pl.ds(start, 8), :] = acc
        return carry

    lax.fori_loop(0, n_date // 8, date_body, 0)

    sub = lax.broadcasted_iota(jnp.int32, (2 * LOOK_R, cols), 0)
    sign = jnp.where(sub < LOOK_R, -1.0, 1.0).astype(jnp.float32)

    def swap_body(d, carry):
        g_ref[d] = pltpu.roll(f_ref[d], LOOK_R, 0) * sign
        return carry

    lax.fori_loop(0, n_date, swap_body, 0)

    masks = {h: (sub & h) == 0 for h in (4, 2, 1)}

    def combine(x, y, h):
        m = masks[h]
        w = jnp.where(m, y, x)
        if h == 4:
            moved = pltpu.roll(w, 4, 0)
        else:
            moved = jnp.where(m, pltpu.roll(w, 8 - h, 0), pltpu.roll(w, h, 0))
        return jnp.where(m, x, y) + moved

    def pair_body(g, carry):
        level = []
        for i in (0, 4, 2, 6, 1, 5, 3, 7):
            p = g * 8 + i
            level.append(f_ref[pairs_s[p, 0]] * g_ref[pairs_s[p, 1]])
        for h in (4, 2, 1):
            level = [combine(level[2 * j], level[2 * j + 1], h) for j in range(len(level) // 2)]
        start = pl.multiple_of(g * 8, 8)
        rows_ref[pl.ds(start, 8), :] = level[0]
        return carry

    lax.fori_loop(0, n_pair // 8, pair_body, 0)

    c_idx = lax.broadcasted_iota(jnp.int32, (cols, looks), 0)
    j_idx = lax.broadcasted_iota(jnp.int32, (cols, looks), 1)
    window = ((c_idx >= j_idx * LOOK_C) & (c_idx < j_idx * LOOK_C + LOOK_C)).astype(jnp.bfloat16)
    looked = dot3(split3(rows_ref[...]), window, True)
    looked_cross = looked[0:n_pair]
    looked_pow = looked[n_pair:n_pair + n_date]

    date_idx = lax.broadcasted_iota(jnp.int32, (n_pair, n_date), 1)
    sel_a = (pairs_v[:, 0:1] == date_idx).astype(jnp.bfloat16)
    sel_b = (pairs_v[:, 1:2] == date_idx).astype(jnp.bfloat16)
    pow_parts = split3(looked_pow)
    looked_ref = dot3(pow_parts, sel_a, False)
    looked_sec = dot3(pow_parts, sel_b, False)

    proxy = looked_cross / jnp.sqrt(looked_ref * looked_sec + 1e-06)
    series = dot3(split3(proxy), inv_ref[...], False)
    for s in range(series.shape[0]):
        out_ref[s] = series[s:s + 1, :]


def regroup_kernel(in_ref, out_ref):
    for c in range(out_ref.shape[0]):
        for k in range(2):
            out_ref[c, k] = in_ref[k, c * LOOK_R:(c + 1) * LOOK_R, :]


def per_device(slc, pairs, inverse):
    n_date = lax.axis_size("date")
    n_pair = pairs.shape[0]
    steps = inverse.shape[0]
    _, _, all_rows, cols = slc.shape
    rows = all_rows // n_date
    chunks = pl.pallas_call(
        regroup_kernel,
        out_shape=jax.ShapeDtypeStruct((n_date, 2, rows, cols), slc.dtype),
        in_specs=[pl.BlockSpec(memory_space=pltpu.VMEM)],
        out_specs=pl.BlockSpec(memory_space=pltpu.VMEM),
    )(slc[0])
    stripes = lax.all_to_all(chunks, "date", split_axis=0, concat_axis=0, tiled=True)
    assert rows == LOOK_R and n_date % 8 == 0 and n_pair % 8 == 0
    looks = cols // LOOK_C
    out = pl.pallas_call(
        functools.partial(kernel, n_date, n_pair),
        out_shape=jax.ShapeDtypeStruct((steps, 1, looks), jnp.float32),
        in_specs=[
            pl.BlockSpec(memory_space=pltpu.SMEM),
            pl.BlockSpec(memory_space=pltpu.VMEM),
            pl.BlockSpec(memory_space=pl.ANY),
            pl.BlockSpec(memory_space=pltpu.VMEM),
        ],
        out_specs=pl.BlockSpec(memory_space=pltpu.VMEM),
        scratch_shapes=[
            pltpu.VMEM((n_date, 2 * LOOK_R, cols), jnp.float32),
            pltpu.VMEM((n_date, 2 * LOOK_R, cols), jnp.float32),
            pltpu.VMEM((n_pair + n_date, cols), jnp.float32),
            pltpu.VMEM(stripes.shape, stripes.dtype),
        ],
        compiler_params=pltpu.CompilerParams(vmem_limit_bytes=24 * 1024 * 1024),
    )(pairs, pairs, stripes, inverse)
    return out


def solution(mesh):
    in_specs = (P("date", None, "grp", None), P(), P())
    out_specs = P(None, ("grp", "date"), None)
    return jax.shard_map(
        per_device, mesh=mesh, in_specs=in_specs, out_specs=out_specs, check_vma=False
    )
```

```python
import functools

import jax
import jax.numpy as jnp
from jax import lax
from jax.experimental import pallas as pl
from jax.experimental.pallas import tpu as pltpu
from jax.sharding import PartitionSpec as P

LOOK_R = 4
LOOK_C = 16


def split3(x):
    hi = x.astype(jnp.bfloat16)
    rest = x - hi.astype(jnp.float32)
    mid = rest.astype(jnp.bfloat16)
    lo = (rest - mid.astype(jnp.float32)).astype(jnp.bfloat16)
    return hi, mid, lo


def dot3(parts, w, lhs_is_split):
    out = None
    for part in parts:
        if lhs_is_split:
            term = jnp.dot(part, w, preferred_element_type=jnp.float32)
        else:
            term = jnp.dot(w, part, preferred_element_type=jnp.float32)
        out = term if out is None else out + term
    return out


def kernel(n_date, n_pair, pairs_s, pairs_v, st_ref, inv_ref, out_ref, f_ref, g_ref, rows_ref):
    cols = st_ref.shape[-1]
    looks = cols // LOOK_C

    def date_body(g, carry):
        acc = jnp.zeros((8, cols), jnp.float32)
        sub = lax.broadcasted_iota(jnp.int32, (8, cols), 0)
        for i in range(8):
            d = g * 8 + i
            re = st_ref[d, 0].astype(jnp.float32)
            im = st_ref[d, 1].astype(jnp.float32)
            f_ref[d, 0:LOOK_R, :] = re
            f_ref[d, LOOK_R:2 * LOOK_R, :] = im
            row = jnp.sum(re * re + im * im, axis=0, keepdims=True)
            acc = jnp.where(sub == i, jnp.broadcast_to(row, (8, cols)), acc)
        start = pl.multiple_of(n_pair + g * 8, 8)
        rows_ref[pl.ds(start, 8), :] = acc
        return carry

    lax.fori_loop(0, n_date // 8, date_body, 0)

    sub = lax.broadcasted_iota(jnp.int32, (2 * LOOK_R, cols), 0)
    sign = jnp.where(sub < LOOK_R, -1.0, 1.0).astype(jnp.float32)

    def swap_body(d, carry):
        g_ref[d] = pltpu.roll(f_ref[d], LOOK_R, 0) * sign
        return carry

    lax.fori_loop(0, n_date, swap_body, 0)

    masks = {h: (sub & h) == 0 for h in (4, 2, 1)}

    def combine(x, y, h):
        m = masks[h]
        w = jnp.where(m, y, x)
        if h == 4:
            moved = pltpu.roll(w, 4, 0)
        else:
            moved = jnp.where(m, pltpu.roll(w, 8 - h, 0), pltpu.roll(w, h, 0))
        return jnp.where(m, x, y) + moved

    def pair_body(g, carry):
        level = []
        for i in (0, 4, 2, 6, 1, 5, 3, 7):
            p = g * 8 + i
            level.append(f_ref[pairs_s[p, 0]] * g_ref[pairs_s[p, 1]])
        for h in (4, 2, 1):
            level = [combine(level[2 * j], level[2 * j + 1], h) for j in range(len(level) // 2)]
        start = pl.multiple_of(g * 8, 8)
        rows_ref[pl.ds(start, 8), :] = level[0]
        return carry

    lax.fori_loop(0, n_pair // 8, pair_body, 0)

    c_idx = lax.broadcasted_iota(jnp.int32, (cols, looks), 0)
    j_idx = lax.broadcasted_iota(jnp.int32, (cols, looks), 1)
    window = ((c_idx >= j_idx * LOOK_C) & (c_idx < j_idx * LOOK_C + LOOK_C)).astype(jnp.bfloat16)
    looked = dot3(split3(rows_ref[...]), window, True)
    looked_cross = looked[0:n_pair]
    looked_pow = looked[n_pair:n_pair + n_date]

    date_idx = lax.broadcasted_iota(jnp.int32, (n_pair, n_date), 1)
    sel_a = (pairs_v[:, 0:1] == date_idx).astype(jnp.bfloat16)
    sel_b = (pairs_v[:, 1:2] == date_idx).astype(jnp.bfloat16)
    pow_parts = split3(looked_pow)
    looked_ref = dot3(pow_parts, sel_a, False)
    looked_sec = dot3(pow_parts, sel_b, False)

    proxy = looked_cross / jnp.sqrt(looked_ref * looked_sec + 1e-06)
    series = dot3(split3(proxy), inv_ref[...], False)
    for s in range(series.shape[0]):
        out_ref[s] = series[s:s + 1, :]


def regroup_kernel(in_ref, out_ref):
    for c in range(out_ref.shape[0]):
        for k in range(2):
            out_ref[c, k] = in_ref[k, c * LOOK_R:(c + 1) * LOOK_R, :]


def per_device(slc, pairs, inverse):
    n_date = lax.axis_size("date")
    n_pair = pairs.shape[0]
    steps = inverse.shape[0]
    _, _, all_rows, cols = slc.shape
    rows = all_rows // n_date
    chunks = pl.pallas_call(
        regroup_kernel,
        out_shape=jax.ShapeDtypeStruct((n_date, 2, rows, cols), slc.dtype),
        in_specs=[pl.BlockSpec(memory_space=pltpu.VMEM)],
        out_specs=pl.BlockSpec(memory_space=pltpu.VMEM),
        compiler_params=pltpu.CompilerParams(vmem_limit_bytes=8 * 1024 * 1024),
    )(slc[0])
    stripes = lax.all_to_all(chunks, "date", split_axis=0, concat_axis=0, tiled=True)
    assert rows == LOOK_R and n_date % 8 == 0 and n_pair % 8 == 0
    looks = cols // LOOK_C
    out = pl.pallas_call(
        functools.partial(kernel, n_date, n_pair),
        out_shape=jax.ShapeDtypeStruct((steps, 1, looks), jnp.float32),
        in_specs=[
            pl.BlockSpec(memory_space=pltpu.SMEM),
            pl.BlockSpec(memory_space=pltpu.VMEM),
            pl.BlockSpec(memory_space=pltpu.VMEM),
            pl.BlockSpec(memory_space=pltpu.VMEM),
        ],
        out_specs=pl.BlockSpec(memory_space=pltpu.VMEM),
        scratch_shapes=[
            pltpu.VMEM((n_date, 2 * LOOK_R, cols), jnp.float32),
            pltpu.VMEM((n_date, 2 * LOOK_R, cols), jnp.float32),
            pltpu.VMEM((n_pair + n_date, cols), jnp.float32),
        ],
        compiler_params=pltpu.CompilerParams(vmem_limit_bytes=24 * 1024 * 1024),
    )(pairs, pairs, stripes, inverse)
    return out


def solution(mesh):
    in_specs = (P("date", None, "grp", None), P(), P())
    out_specs = P(None, ("grp", "date"), None)
    return jax.shard_map(
        per_device, mesh=mesh, in_specs=in_specs, out_specs=out_specs, check_vma=False
    )
```

```python
import functools

import jax
import jax.numpy as jnp
from jax import lax
from jax.experimental import pallas as pl
from jax.experimental.pallas import tpu as pltpu
from jax.sharding import PartitionSpec as P

LOOK_R = 4
LOOK_C = 16


def split3(x):
    hi = x.astype(jnp.bfloat16)
    rest = x - hi.astype(jnp.float32)
    mid = rest.astype(jnp.bfloat16)
    lo = (rest - mid.astype(jnp.float32)).astype(jnp.bfloat16)
    return hi, mid, lo


def dot3(parts, w, lhs_is_split):
    out = None
    for part in parts:
        if lhs_is_split:
            term = jnp.dot(part, w, preferred_element_type=jnp.float32)
        else:
            term = jnp.dot(w, part, preferred_element_type=jnp.float32)
        out = term if out is None else out + term
    return out


def kernel(n_date, n_pair, pairs_s, pairs_v, st_ref, inv_ref, window_ref, out_ref, f_ref, g_ref, rows_ref):
    cols = st_ref.shape[-1]
    looks = cols // LOOK_C

    def date_body(d, carry):
        f_ref[d, 0:LOOK_R, :] = st_ref[d, 0].astype(jnp.float32)
        f_ref[d, LOOK_R:2 * LOOK_R, :] = st_ref[d, 1].astype(jnp.float32)
        return carry

    lax.fori_loop(0, n_date, date_body, 0)

    sub = lax.broadcasted_iota(jnp.int32, (2 * LOOK_R, cols), 0)
    sign = jnp.where(sub < LOOK_R, -1.0, 1.0).astype(jnp.float32)

    def swap_body(d, carry):
        g_ref[d] = pltpu.roll(f_ref[d], LOOK_R, 0) * sign
        return carry

    lax.fori_loop(0, n_date, swap_body, 0)

    masks = {h: (sub & h) == 0 for h in (4, 2, 1)}

    def combine(x, y, h):
        m = masks[h]
        w = jnp.where(m, y, x)
        if h == 4:
            moved = pltpu.roll(w, 4, 0)
        else:
            moved = jnp.where(m, pltpu.roll(w, 8 - h, 0), pltpu.roll(w, h, 0))
        return jnp.where(m, x, y) + moved

    def power_body(g, carry):
        level = []
        for i in (0, 4, 2, 6, 1, 5, 3, 7):
            x = f_ref[g * 8 + i]
            level.append(x * x)
        for h in (4, 2, 1):
            level = [combine(level[2 * j], level[2 * j + 1], h) for j in range(len(level) // 2)]
        start = pl.multiple_of(n_pair + g * 8, 8)
        rows_ref[pl.ds(start, 8), :] = level[0]
        return carry

    lax.fori_loop(0, n_date // 8, power_body, 0)

    def pair_body(g, carry):
        level = []
        for i in (0, 4, 2, 6, 1, 5, 3, 7):
            p = g * 8 + i
            level.append(f_ref[pairs_s[p, 0]] * g_ref[pairs_s[p, 1]])
        for h in (4, 2, 1):
            level = [combine(level[2 * j], level[2 * j + 1], h) for j in range(len(level) // 2)]
        start = pl.multiple_of(g * 8, 8)
        rows_ref[pl.ds(start, 8), :] = level[0]
        return carry

    lax.fori_loop(0, n_pair // 8, pair_body, 0)

    looked = dot3(split3(rows_ref[...]), window_ref[...], True)
    looked_cross = looked[0:n_pair]
    looked_pow = looked[n_pair:n_pair + n_date]

    date_idx = lax.broadcasted_iota(jnp.int32, (n_pair, n_date), 1)
    sel_a = (pairs_v[:, 0:1] == date_idx).astype(jnp.bfloat16)
    sel_b = (pairs_v[:, 1:2] == date_idx).astype(jnp.bfloat16)
    pow_parts = split3(looked_pow)
    looked_ref = dot3(pow_parts, sel_a, False)
    looked_sec = dot3(pow_parts, sel_b, False)

    proxy = looked_cross / jnp.sqrt(looked_ref * looked_sec + 1e-06)
    series = dot3(split3(proxy), inv_ref[...], False)
    for s in range(series.shape[0]):
        out_ref[s] = series[s:s + 1, :]


def regroup_kernel(in_ref, out_ref):
    for c in range(out_ref.shape[0]):
        for k in range(2):
            out_ref[c, k] = in_ref[k, c * LOOK_R:(c + 1) * LOOK_R, :]


def per_device(slc, pairs, inverse):
    n_date = lax.axis_size("date")
    n_pair = pairs.shape[0]
    steps = inverse.shape[0]
    _, _, all_rows, cols = slc.shape
    rows = all_rows // n_date
    chunks = pl.pallas_call(
        regroup_kernel,
        out_shape=jax.ShapeDtypeStruct((n_date, 2, rows, cols), slc.dtype),
        in_specs=[pl.BlockSpec(memory_space=pltpu.VMEM)],
        out_specs=pl.BlockSpec(memory_space=pltpu.VMEM),
        compiler_params=pltpu.CompilerParams(vmem_limit_bytes=8 * 1024 * 1024),
    )(slc[0])
    stripes = lax.all_to_all(chunks, "date", split_axis=0, concat_axis=0, tiled=True)
    assert rows == LOOK_R and n_date % 8 == 0 and n_pair % 8 == 0
    looks = cols // LOOK_C
    col = lax.broadcasted_iota(jnp.int32, (cols, looks), 0) // LOOK_C
    window = (col == lax.broadcasted_iota(jnp.int32, (cols, looks), 1)).astype(jnp.bfloat16)
    out = pl.pallas_call(
        functools.partial(kernel, n_date, n_pair),
        out_shape=jax.ShapeDtypeStruct((steps, 1, looks), jnp.float32),
        in_specs=[
            pl.BlockSpec(memory_space=pltpu.SMEM),
            pl.BlockSpec(memory_space=pltpu.VMEM),
            pl.BlockSpec(memory_space=pltpu.VMEM),
            pl.BlockSpec(memory_space=pltpu.VMEM),
            pl.BlockSpec(memory_space=pltpu.VMEM),
        ],
        out_specs=pl.BlockSpec(memory_space=pltpu.VMEM),
        scratch_shapes=[
            pltpu.VMEM((n_date, 2 * LOOK_R, cols), jnp.float32),
            pltpu.VMEM((n_date, 2 * LOOK_R, cols), jnp.float32),
            pltpu.VMEM((n_pair + n_date, cols), jnp.float32),
        ],
        compiler_params=pltpu.CompilerParams(vmem_limit_bytes=24 * 1024 * 1024),
    )(pairs, pairs, stripes, inverse, window)
    return out


def solution(mesh):
    in_specs = (P("date", None, "grp", None), P(), P())
    out_specs = P(None, ("grp", "date"), None)
    return jax.shard_map(
        per_device, mesh=mesh, in_specs=in_specs, out_specs=out_specs, check_vma=False
    )
```

```python
import functools

import jax
import jax.numpy as jnp
from jax import lax
from jax.experimental import pallas as pl
from jax.experimental.pallas import tpu as pltpu
from jax.sharding import PartitionSpec as P

LOOK_R = 4
LOOK_C = 16


def split3(x):
    hi = x.astype(jnp.bfloat16)
    rest = x - hi.astype(jnp.float32)
    mid = rest.astype(jnp.bfloat16)
    lo = (rest - mid.astype(jnp.float32)).astype(jnp.bfloat16)
    return hi, mid, lo


def dot3(parts, w, lhs_is_split):
    out = None
    for part in parts:
        if lhs_is_split:
            term = jnp.dot(part, w, preferred_element_type=jnp.float32)
        else:
            term = jnp.dot(w, part, preferred_element_type=jnp.float32)
        out = term if out is None else out + term
    return out


def kernel(n_date, n_pair, pairs_s, pairs_v, st_ref, inv_ref, window_ref, out_ref, f_ref, g_ref, rows_ref):
    cols = st_ref.shape[-1]
    looks = cols // LOOK_C

    def date_body(d, carry):
        f_ref[d] = st_ref[d].astype(jnp.float32)
        return carry

    lax.fori_loop(0, n_date, date_body, 0)

    sub = lax.broadcasted_iota(jnp.int32, (2 * LOOK_R, cols), 0)
    sign = jnp.where(sub < LOOK_R, -1.0, 1.0).astype(jnp.float32)

    def swap_body(d, carry):
        g_ref[d] = pltpu.roll(f_ref[d], LOOK_R, 0) * sign
        return carry

    lax.fori_loop(0, n_date, swap_body, 0)

    masks = {h: (sub & h) == 0 for h in (4, 2, 1)}

    def combine(x, y, h):
        m = masks[h]
        w = jnp.where(m, y, x)
        if h == 4:
            moved = pltpu.roll(w, 4, 0)
        else:
            moved = jnp.where(m, pltpu.roll(w, 8 - h, 0), pltpu.roll(w, h, 0))
        return jnp.where(m, x, y) + moved

    def power_body(g, carry):
        level = []
        for i in (0, 4, 2, 6, 1, 5, 3, 7):
            x = f_ref[g * 8 + i]
            level.append(x * x)
        for h in (4, 2, 1):
            level = [combine(level[2 * j], level[2 * j + 1], h) for j in range(len(level) // 2)]
        start = pl.multiple_of(n_pair + g * 8, 8)
        rows_ref[pl.ds(start, 8), :] = level[0]
        return carry

    lax.fori_loop(0, n_date // 8, power_body, 0)

    def pair_body(g, carry):
        level = []
        for i in (0, 4, 2, 6, 1, 5, 3, 7):
            p = g * 8 + i
            level.append(f_ref[pairs_s[p, 0]] * g_ref[pairs_s[p, 1]])
        for h in (4, 2, 1):
            level = [combine(level[2 * j], level[2 * j + 1], h) for j in range(len(level) // 2)]
        start = pl.multiple_of(g * 8, 8)
        rows_ref[pl.ds(start, 8), :] = level[0]
        return carry

    lax.fori_loop(0, n_pair // 8, pair_body, 0)

    looked = dot3(split3(rows_ref[...]), window_ref[...], True)
    looked_cross = looked[0:n_pair]
    looked_pow = looked[n_pair:n_pair + n_date]

    date_idx = lax.broadcasted_iota(jnp.int32, (n_pair, n_date), 1)
    sel_a = (pairs_v[:, 0:1] == date_idx).astype(jnp.bfloat16)
    sel_b = (pairs_v[:, 1:2] == date_idx).astype(jnp.bfloat16)
    pow_parts = split3(looked_pow)
    looked_ref = dot3(pow_parts, sel_a, False)
    looked_sec = dot3(pow_parts, sel_b, False)

    proxy = looked_cross / jnp.sqrt(looked_ref * looked_sec + 1e-06)
    series = dot3(split3(proxy), inv_ref[...], False)
    for s in range(series.shape[0]):
        out_ref[s] = series[s:s + 1, :]


def regroup_kernel(in_ref, out_ref):
    for c in range(out_ref.shape[0]):
        for k in range(2):
            out_ref[c, k * LOOK_R:(k + 1) * LOOK_R, :] = in_ref[k, c * LOOK_R:(c + 1) * LOOK_R, :]


def per_device(slc, pairs, inverse):
    n_date = lax.axis_size("date")
    n_pair = pairs.shape[0]
    steps = inverse.shape[0]
    _, _, all_rows, cols = slc.shape
    rows = all_rows // n_date
    chunks = pl.pallas_call(
        regroup_kernel,
        out_shape=jax.ShapeDtypeStruct((n_date, 2 * rows, cols), slc.dtype),
        in_specs=[pl.BlockSpec(memory_space=pltpu.VMEM)],
        out_specs=pl.BlockSpec(memory_space=pltpu.VMEM),
        compiler_params=pltpu.CompilerParams(vmem_limit_bytes=8 * 1024 * 1024),
    )(slc[0])
    stripes = lax.all_to_all(chunks, "date", split_axis=0, concat_axis=0, tiled=True)
    assert rows == LOOK_R and n_date % 8 == 0 and n_pair % 8 == 0
    looks = cols // LOOK_C
    col = lax.broadcasted_iota(jnp.int32, (cols, looks), 0) // LOOK_C
    window = (col == lax.broadcasted_iota(jnp.int32, (cols, looks), 1)).astype(jnp.bfloat16)
    out = pl.pallas_call(
        functools.partial(kernel, n_date, n_pair),
        out_shape=jax.ShapeDtypeStruct((steps, 1, looks), jnp.float32),
        in_specs=[
            pl.BlockSpec(memory_space=pltpu.SMEM),
            pl.BlockSpec(memory_space=pltpu.VMEM),
            pl.BlockSpec(memory_space=pltpu.VMEM),
            pl.BlockSpec(memory_space=pltpu.VMEM),
            pl.BlockSpec(memory_space=pltpu.VMEM),
        ],
        out_specs=pl.BlockSpec(memory_space=pltpu.VMEM),
        scratch_shapes=[
            pltpu.VMEM((n_date, 2 * LOOK_R, cols), jnp.float32),
            pltpu.VMEM((n_date, 2 * LOOK_R, cols), jnp.float32),
            pltpu.VMEM((n_pair + n_date, cols), jnp.float32),
        ],
        compiler_params=pltpu.CompilerParams(vmem_limit_bytes=24 * 1024 * 1024),
    )(pairs, pairs, stripes, inverse, window)
    return out


def solution(mesh):
    in_specs = (P("date", None, "grp", None), P(), P())
    out_specs = P(None, ("grp", "date"), None)
    return jax.shard_map(
        per_device, mesh=mesh, in_specs=in_specs, out_specs=out_specs, check_vma=False
    )
```

```python
import functools

import jax
import jax.numpy as jnp
from jax import lax
from jax.experimental import pallas as pl
from jax.experimental.pallas import tpu as pltpu
from jax.sharding import PartitionSpec as P

LOOK_R = 4
LOOK_C = 16


def split3(x):
    hi = x.astype(jnp.bfloat16)
    rest = x - hi.astype(jnp.float32)
    mid = rest.astype(jnp.bfloat16)
    lo = (rest - mid.astype(jnp.float32)).astype(jnp.bfloat16)
    return hi, mid, lo


def dot3(parts, w, lhs_is_split):
    out = None
    for part in parts:
        if lhs_is_split:
            term = jnp.dot(part, w, preferred_element_type=jnp.float32)
        else:
            term = jnp.dot(w, part, preferred_element_type=jnp.float32)
        out = term if out is None else out + term
    return out


def kernel(n_date, n_pair, pairs_s, pairs_v, st_ref, inv_ref, window_ref, out_ref, f_ref, g_ref, rows_ref):
    cols = st_ref.shape[-1]
    looks = cols // LOOK_C

    def date_body(d, carry):
        f_ref[d] = st_ref[d].astype(jnp.float32)
        return carry

    lax.fori_loop(0, n_date, date_body, 0)

    sub = lax.broadcasted_iota(jnp.int32, (2 * LOOK_R, cols), 0)
    sign = jnp.where(sub < LOOK_R, -1.0, 1.0).astype(jnp.float32)

    def swap_body(d, carry):
        g_ref[d] = pltpu.roll(f_ref[d], LOOK_R, 0) * sign
        return carry

    lax.fori_loop(0, n_date, swap_body, 0)

    masks = {h: (sub & h) == 0 for h in (4, 2, 1)}

    def combine(x, y, h):
        m = masks[h]
        w = jnp.where(m, y, x)
        if h == 4:
            moved = pltpu.roll(w, 4, 0)
        else:
            moved = jnp.where(m, pltpu.roll(w, 8 - h, 0), pltpu.roll(w, h, 0))
        return jnp.where(m, x, y) + moved

    def power_body(g, carry):
        level = []
        for i in (0, 4, 2, 6, 1, 5, 3, 7):
            x = f_ref[g * 8 + i]
            level.append(x * x)
        for h in (4, 2, 1):
            level = [combine(level[2 * j], level[2 * j + 1], h) for j in range(len(level) // 2)]
        start = pl.multiple_of(n_pair + g * 8, 8)
        rows_ref[pl.ds(start, 8), :] = level[0]
        return carry

    lax.fori_loop(0, n_date // 8, power_body, 0)

    def pair_body(g, carry):
        level = []
        for i in (0, 4, 2, 6, 1, 5, 3, 7):
            p = g * 8 + i
            level.append(f_ref[pairs_s[p, 0]] * g_ref[pairs_s[p, 1]])
        for h in (4, 2, 1):
            level = [combine(level[2 * j], level[2 * j + 1], h) for j in range(len(level) // 2)]
        start = pl.multiple_of(g * 8, 8)
        rows_ref[pl.ds(start, 8), :] = level[0]
        return carry

    lax.fori_loop(0, n_pair // 8, pair_body, 0)

    looked = dot3(split3(rows_ref[...]), window_ref[...], True)
    looked_cross = looked[0:n_pair]
    looked_pow = looked[n_pair:n_pair + n_date]

    date_idx = lax.broadcasted_iota(jnp.int32, (n_pair, n_date), 1)
    sel_a = (pairs_v[:, 0:1] == date_idx).astype(jnp.bfloat16)
    sel_b = (pairs_v[:, 1:2] == date_idx).astype(jnp.bfloat16)
    pow_parts = split3(looked_pow)
    looked_ref = dot3(pow_parts, sel_a, False)
    looked_sec = dot3(pow_parts, sel_b, False)

    proxy = looked_cross / jnp.sqrt(looked_ref * looked_sec + 1e-06)
    series = dot3(split3(proxy), inv_ref[...], False)
    for s in range(series.shape[0]):
        out_ref[s] = series[s:s + 1, :]


def regroup_kernel(in_hbm, out_ref, in_ref, sems):
    n_chunk = out_ref.shape[0]
    half = n_chunk // 2
    rows_half = half * LOOK_R
    copies = []
    for k in range(2):
        for q in range(2):
            rows = pl.ds(q * rows_half, rows_half)
            copy = pltpu.make_async_copy(in_hbm.at[k, rows], in_ref.at[k, rows], sems.at[2 * k + q])
            copy.start()
            copies.append(copy)
    for k in range(2):
        for q in range(2):
            copies[2 * k + q].wait()
            for c in range(q * half, (q + 1) * half):
                out_ref[c, k * LOOK_R:(k + 1) * LOOK_R, :] = in_ref[k, c * LOOK_R:(c + 1) * LOOK_R, :]


def per_device(slc, pairs, inverse):
    n_date = lax.axis_size("date")
    n_pair = pairs.shape[0]
    steps = inverse.shape[0]
    _, _, all_rows, cols = slc.shape
    rows = all_rows // n_date
    chunks = pl.pallas_call(
        regroup_kernel,
        out_shape=jax.ShapeDtypeStruct((n_date, 2 * rows, cols), slc.dtype),
        in_specs=[pl.BlockSpec(memory_space=pl.ANY)],
        out_specs=pl.BlockSpec(memory_space=pltpu.VMEM),
        scratch_shapes=[pltpu.VMEM(slc.shape[1:], slc.dtype), pltpu.SemaphoreType.DMA((4,))],
    )(slc[0])
    stripes = lax.all_to_all(chunks, "date", split_axis=0, concat_axis=0, tiled=True)
    assert rows == LOOK_R and n_date % 8 == 0 and n_pair % 8 == 0
    looks = cols // LOOK_C
    col = lax.broadcasted_iota(jnp.int32, (cols, looks), 0) // LOOK_C
    window = (col == lax.broadcasted_iota(jnp.int32, (cols, looks), 1)).astype(jnp.bfloat16)
    out = pl.pallas_call(
        functools.partial(kernel, n_date, n_pair),
        out_shape=jax.ShapeDtypeStruct((steps, 1, looks), jnp.float32),
        in_specs=[
            pl.BlockSpec(memory_space=pltpu.SMEM),
            pl.BlockSpec(memory_space=pltpu.VMEM),
            pl.BlockSpec(memory_space=pltpu.VMEM),
            pl.BlockSpec(memory_space=pltpu.VMEM),
            pl.BlockSpec(memory_space=pltpu.VMEM),
        ],
        out_specs=pl.BlockSpec(memory_space=pltpu.VMEM),
        scratch_shapes=[
            pltpu.VMEM((n_date, 2 * LOOK_R, cols), jnp.float32),
            pltpu.VMEM((n_date, 2 * LOOK_R, cols), jnp.float32),
            pltpu.VMEM((n_pair + n_date, cols), jnp.float32),
        ],
        compiler_params=pltpu.CompilerParams(vmem_limit_bytes=24 * 1024 * 1024),
    )(pairs, pairs, stripes, inverse, window)
    return out


def solution(mesh):
    in_specs = (P("date", None, "grp", None), P(), P())
    out_specs = P(None, ("grp", "date"), None)
    return jax.shard_map(
        per_device, mesh=mesh, in_specs=in_specs, out_specs=out_specs, check_vma=False
    )
```

```python
import functools

import jax
import jax.numpy as jnp
from jax import lax
from jax.experimental import pallas as pl
from jax.experimental.pallas import tpu as pltpu
from jax.sharding import PartitionSpec as P

LOOK_R = 4
LOOK_C = 16


def split3(x):
    hi = x.astype(jnp.bfloat16)
    rest = x - hi.astype(jnp.float32)
    mid = rest.astype(jnp.bfloat16)
    lo = (rest - mid.astype(jnp.float32)).astype(jnp.bfloat16)
    return hi, mid, lo


def dot3(parts, w, lhs_is_split):
    out = None
    for part in parts:
        if lhs_is_split:
            term = jnp.dot(part, w, preferred_element_type=jnp.float32)
        else:
            term = jnp.dot(w, part, preferred_element_type=jnp.float32)
        out = term if out is None else out + term
    return out


def kernel(n_date, n_pair, pairs_s, pairs_v, st_ref, inv_ref, window_ref, out_ref, f_ref, g_ref, rows_ref):
    cols = st_ref.shape[-1]
    looks = cols // LOOK_C

    def date_body(d, carry):
        f_ref[d] = st_ref[d].astype(jnp.float32)
        return carry

    lax.fori_loop(0, n_date, date_body, 0)

    sub = lax.broadcasted_iota(jnp.int32, (2 * LOOK_R, cols), 0)
    sign = jnp.where(sub < LOOK_R, -1.0, 1.0).astype(jnp.float32)

    def swap_body(d, carry):
        g_ref[d] = pltpu.roll(f_ref[d], LOOK_R, 0) * sign
        return carry

    lax.fori_loop(0, n_date, swap_body, 0)

    masks = {h: (sub & h) == 0 for h in (4, 2, 1)}

    def combine(x, y, h):
        m = masks[h]
        w = jnp.where(m, y, x)
        if h == 4:
            moved = pltpu.roll(w, 4, 0)
        else:
            moved = jnp.where(m, pltpu.roll(w, 8 - h, 0), pltpu.roll(w, h, 0))
        return jnp.where(m, x, y) + moved

    def power_body(g, carry):
        level = []
        for i in (0, 4, 2, 6, 1, 5, 3, 7):
            x = f_ref[g * 8 + i]
            level.append(x * x)
        for h in (4, 2, 1):
            level = [combine(level[2 * j], level[2 * j + 1], h) for j in range(len(level) // 2)]
        start = pl.multiple_of(n_pair + g * 8, 8)
        rows_ref[pl.ds(start, 8), :] = level[0]
        return carry

    lax.fori_loop(0, n_date // 8, power_body, 0)

    def pair_body(g, carry):
        level = []
        for i in (0, 4, 2, 6, 1, 5, 3, 7):
            p = g * 8 + i
            level.append(f_ref[pairs_s[p, 0]] * g_ref[pairs_s[p, 1]])
        for h in (4, 2, 1):
            level = [combine(level[2 * j], level[2 * j + 1], h) for j in range(len(level) // 2)]
        start = pl.multiple_of(g * 8, 8)
        rows_ref[pl.ds(start, 8), :] = level[0]
        return carry

    lax.fori_loop(0, n_pair // 8, pair_body, 0)

    looked = dot3(split3(rows_ref[...]), window_ref[...], True)
    looked_cross = looked[0:n_pair]
    looked_pow = looked[n_pair:n_pair + n_date]

    date_idx = lax.broadcasted_iota(jnp.int32, (n_pair, n_date), 1)
    sel_a = (pairs_v[:, 0:1] == date_idx).astype(jnp.bfloat16)
    sel_b = (pairs_v[:, 1:2] == date_idx).astype(jnp.bfloat16)
    pow_parts = split3(looked_pow)
    looked_ref = dot3(pow_parts, sel_a, False)
    looked_sec = dot3(pow_parts, sel_b, False)

    proxy = looked_cross / jnp.sqrt(looked_ref * looked_sec + 1e-06)
    series = dot3(split3(proxy), inv_ref[...], False)
    for s in range(series.shape[0]):
        out_ref[s] = series[s:s + 1, :]


def regroup_kernel(in_hbm, out_a, out_b, in_ref, sems):
    n_chunk = out_a.shape[0]
    width = out_a.shape[-1]
    half = n_chunk // 2
    rows_half = half * LOOK_R
    copies = []
    for k in range(2):
        for q in range(2):
            rows = pl.ds(q * rows_half, rows_half)
            copy = pltpu.make_async_copy(in_hbm.at[k, rows], in_ref.at[k, rows], sems.at[2 * k + q])
            copy.start()
            copies.append(copy)
    for k in range(2):
        for q in range(2):
            copies[2 * k + q].wait()
            for c in range(q * half, (q + 1) * half):
                block = in_ref[k, c * LOOK_R:(c + 1) * LOOK_R, :]
                out_a[c, k * LOOK_R:(k + 1) * LOOK_R, :] = block[:, 0:width]
                out_b[c, k * LOOK_R:(k + 1) * LOOK_R, :] = block[:, width:2 * width]


def per_device(slc, pairs, inverse):
    n_date = lax.axis_size("date")
    n_pair = pairs.shape[0]
    steps = inverse.shape[0]
    _, _, all_rows, cols = slc.shape
    rows = all_rows // n_date
    width = cols // 2
    halves = pl.pallas_call(
        regroup_kernel,
        out_shape=[jax.ShapeDtypeStruct((n_date, 2 * rows, width), slc.dtype)] * 2,
        in_specs=[pl.BlockSpec(memory_space=pl.ANY)],
        out_specs=[pl.BlockSpec(memory_space=pltpu.VMEM)] * 2,
        scratch_shapes=[pltpu.VMEM(slc.shape[1:], slc.dtype), pltpu.SemaphoreType.DMA((4,))],
    )(slc[0])
    stripes = [lax.all_to_all(h, "date", split_axis=0, concat_axis=0, tiled=True) for h in halves]
    assert rows == LOOK_R and n_date % 8 == 0 and n_pair % 8 == 0
    looks = width // LOOK_C
    col = lax.broadcasted_iota(jnp.int32, (width, looks), 0) // LOOK_C
    window = (col == lax.broadcasted_iota(jnp.int32, (width, looks), 1)).astype(jnp.bfloat16)
    outs = [pl.pallas_call(
        functools.partial(kernel, n_date, n_pair),
        out_shape=jax.ShapeDtypeStruct((steps, 1, looks), jnp.float32),
        in_specs=[
            pl.BlockSpec(memory_space=pltpu.SMEM),
            pl.BlockSpec(memory_space=pltpu.VMEM),
            pl.BlockSpec(memory_space=pltpu.VMEM),
            pl.BlockSpec(memory_space=pltpu.VMEM),
            pl.BlockSpec(memory_space=pltpu.VMEM),
        ],
        out_specs=pl.BlockSpec(memory_space=pltpu.VMEM),
        scratch_shapes=[
            pltpu.VMEM((n_date, 2 * LOOK_R, width), jnp.float32),
            pltpu.VMEM((n_date, 2 * LOOK_R, width), jnp.float32),
            pltpu.VMEM((n_pair + n_date, width), jnp.float32),
        ],
        compiler_params=pltpu.CompilerParams(vmem_limit_bytes=24 * 1024 * 1024),
    )(pairs, pairs, st, inverse, window) for st in stripes]
    return jnp.concatenate(outs, axis=2)


def solution(mesh):
    in_specs = (P("date", None, "grp", None), P(), P())
    out_specs = P(None, ("grp", "date"), None)
    return jax.shard_map(
        per_device, mesh=mesh, in_specs=in_specs, out_specs=out_specs, check_vma=False
    )
```

```python
import functools

import jax
import jax.numpy as jnp
from jax import lax
from jax.experimental import pallas as pl
from jax.experimental.pallas import tpu as pltpu
from jax.sharding import PartitionSpec as P

LOOK_R = 4
LOOK_C = 16


def split3(x):
    hi = x.astype(jnp.bfloat16)
    rest = x - hi.astype(jnp.float32)
    mid = rest.astype(jnp.bfloat16)
    lo = (rest - mid.astype(jnp.float32)).astype(jnp.bfloat16)
    return hi, mid, lo


def dot3(parts, w, lhs_is_split):
    out = None
    for part in parts:
        if lhs_is_split:
            term = jnp.dot(part, w, preferred_element_type=jnp.float32)
        else:
            term = jnp.dot(w, part, preferred_element_type=jnp.float32)
        out = term if out is None else out + term
    return out


def kernel(n_date, n_pair, pairs_s, pairs_v, st_ref, inv_ref, window_ref, out_ref, f_ref, g_ref, rows_ref):
    cols = st_ref.shape[-1]
    looks = cols // LOOK_C

    def date_body(d, carry):
        f_ref[d] = st_ref[d].astype(jnp.float32)
        return carry

    lax.fori_loop(0, n_date, date_body, 0)

    sub = lax.broadcasted_iota(jnp.int32, (2 * LOOK_R, cols), 0)
    sign = jnp.where(sub < LOOK_R, -1.0, 1.0).astype(jnp.float32)

    def swap_body(d, carry):
        g_ref[d] = pltpu.roll(f_ref[d], LOOK_R, 0) * sign
        return carry

    lax.fori_loop(0, n_date, swap_body, 0)

    masks = {h: (sub & h) == 0 for h in (4, 2, 1)}

    def combine(x, y, h):
        m = masks[h]
        w = jnp.where(m, y, x)
        if h == 4:
            moved = pltpu.roll(w, 4, 0)
        else:
            moved = jnp.where(m, pltpu.roll(w, 8 - h, 0), pltpu.roll(w, h, 0))
        return jnp.where(m, x, y) + moved

    def power_body(g, carry):
        level = []
        for i in (0, 4, 2, 6, 1, 5, 3, 7):
            x = f_ref[g * 8 + i]
            level.append(x * x)
        for h in (4, 2, 1):
            level = [combine(level[2 * j], level[2 * j + 1], h) for j in range(len(level) // 2)]
        start = pl.multiple_of(n_pair + g * 8, 8)
        rows_ref[pl.ds(start, 8), :] = level[0]
        return carry

    lax.fori_loop(0, n_date // 8, power_body, 0)

    def pair_body(g, carry):
        level = []
        for i in (0, 4, 2, 6, 1, 5, 3, 7):
            p = g * 8 + i
            level.append(f_ref[pairs_s[p, 0]] * g_ref[pairs_s[p, 1]])
        for h in (4, 2, 1):
            level = [combine(level[2 * j], level[2 * j + 1], h) for j in range(len(level) // 2)]
        start = pl.multiple_of(g * 8, 8)
        rows_ref[pl.ds(start, 8), :] = level[0]
        return carry

    lax.fori_loop(0, n_pair // 8, pair_body, 0)

    looked = dot3(split3(rows_ref[...]), window_ref[...], True)
    looked_cross = looked[0:n_pair]
    looked_pow = looked[n_pair:n_pair + n_date]

    date_idx = lax.broadcasted_iota(jnp.int32, (n_pair, n_date), 1)
    sel_a = (pairs_v[:, 0:1] == date_idx).astype(jnp.bfloat16)
    sel_b = (pairs_v[:, 1:2] == date_idx).astype(jnp.bfloat16)
    pow_parts = split3(looked_pow)
    looked_ref = dot3(pow_parts, sel_a, False)
    looked_sec = dot3(pow_parts, sel_b, False)

    proxy = looked_cross / jnp.sqrt(looked_ref * looked_sec + 1e-06)
    series = dot3(split3(proxy), inv_ref[...], False)
    for s in range(series.shape[0]):
        out_ref[s] = series[s:s + 1, :]


def regroup_kernel(in_hbm, out_hbm, in_ref, out_ref, sems, out_sems):
    n_chunk = out_ref.shape[0]
    half = n_chunk // 2
    rows_half = half * LOOK_R
    copies = {}
    for q in range(2):
        for k in range(2):
            rows = pl.ds(q * rows_half, rows_half)
            copy = pltpu.make_async_copy(in_hbm.at[k, rows], in_ref.at[k, rows], sems.at[2 * q + k])
            copy.start()
            copies[q, k] = copy
    outs = []
    for q in range(2):
        for k in range(2):
            copies[q, k].wait()
            for c in range(q * half, (q + 1) * half):
                out_ref[c, k * LOOK_R:(k + 1) * LOOK_R, :] = in_ref[k, c * LOOK_R:(c + 1) * LOOK_R, :]
        chunk = pl.ds(q * half, half)
        out = pltpu.make_async_copy(out_ref.at[chunk], out_hbm.at[chunk], out_sems.at[q])
        out.start()
        outs.append(out)
    for out in outs:
        out.wait()


def per_device(slc, pairs, inverse):
    n_date = lax.axis_size("date")
    n_pair = pairs.shape[0]
    steps = inverse.shape[0]
    _, _, all_rows, cols = slc.shape
    rows = all_rows // n_date
    chunks = pl.pallas_call(
        regroup_kernel,
        out_shape=jax.ShapeDtypeStruct((n_date, 2 * rows, cols), slc.dtype),
        in_specs=[pl.BlockSpec(memory_space=pl.ANY)],
        out_specs=pl.BlockSpec(memory_space=pl.ANY),
        scratch_shapes=[
            pltpu.VMEM(slc.shape[1:], slc.dtype),
            pltpu.VMEM((n_date, 2 * rows, cols), slc.dtype),
            pltpu.SemaphoreType.DMA((4,)),
            pltpu.SemaphoreType.DMA((2,)),
        ],
    )(slc[0])
    stripes = lax.all_to_all(chunks, "date", split_axis=0, concat_axis=0, tiled=True)
    assert rows == LOOK_R and n_date % 8 == 0 and n_pair % 8 == 0
    looks = cols // LOOK_C
    col = lax.broadcasted_iota(jnp.int32, (cols, looks), 0) // LOOK_C
    window = (col == lax.broadcasted_iota(jnp.int32, (cols, looks), 1)).astype(jnp.bfloat16)
    out = pl.pallas_call(
        functools.partial(kernel, n_date, n_pair),
        out_shape=jax.ShapeDtypeStruct((steps, 1, looks), jnp.float32),
        in_specs=[
            pl.BlockSpec(memory_space=pltpu.SMEM),
            pl.BlockSpec(memory_space=pltpu.VMEM),
            pl.BlockSpec(memory_space=pltpu.VMEM),
            pl.BlockSpec(memory_space=pltpu.VMEM),
            pl.BlockSpec(memory_space=pltpu.VMEM),
        ],
        out_specs=pl.BlockSpec(memory_space=pltpu.VMEM),
        scratch_shapes=[
            pltpu.VMEM((n_date, 2 * LOOK_R, cols), jnp.float32),
            pltpu.VMEM((n_date, 2 * LOOK_R, cols), jnp.float32),
            pltpu.VMEM((n_pair + n_date, cols), jnp.float32),
        ],
        compiler_params=pltpu.CompilerParams(vmem_limit_bytes=24 * 1024 * 1024),
    )(pairs, pairs, stripes, inverse, window)
    return out


def solution(mesh):
    in_specs = (P("date", None, "grp", None), P(), P())
    out_specs = P(None, ("grp", "date"), None)
    return jax.shard_map(
        per_device, mesh=mesh, in_specs=in_specs, out_specs=out_specs, check_vma=False
    )
```

```python
import functools

import jax
import jax.numpy as jnp
from jax import lax
from jax.experimental import pallas as pl
from jax.experimental.pallas import tpu as pltpu
from jax.sharding import PartitionSpec as P

LOOK_R = 4
LOOK_C = 16


def split3(x):
    hi = x.astype(jnp.bfloat16)
    rest = x - hi.astype(jnp.float32)
    mid = rest.astype(jnp.bfloat16)
    lo = (rest - mid.astype(jnp.float32)).astype(jnp.bfloat16)
    return hi, mid, lo


def dot3(parts, w, lhs_is_split):
    out = None
    for part in parts:
        if lhs_is_split:
            term = jnp.dot(part, w, preferred_element_type=jnp.float32)
        else:
            term = jnp.dot(w, part, preferred_element_type=jnp.float32)
        out = term if out is None else out + term
    return out


def kernel(n_date, n_pair, pairs_s, pairs_v, st_ref, inv_ref, window_ref, out_ref, f_ref, g_ref, rows_ref):
    cols = st_ref.shape[-1]
    looks = cols // LOOK_C

    sub = lax.broadcasted_iota(jnp.int32, (2 * LOOK_R, cols), 0)
    sign = jnp.where(sub < LOOK_R, -1.0, 1.0).astype(jnp.float32)

    def date_body(d, carry):
        x = st_ref[d].astype(jnp.float32)
        f_ref[d] = x
        g_ref[d] = pltpu.roll(x, LOOK_R, 0) * sign
        return carry

    lax.fori_loop(0, n_date, date_body, 0)

    masks = {h: (sub & h) == 0 for h in (4, 2, 1)}

    def combine(x, y, h):
        m = masks[h]
        if h == 4:
            return jnp.where(m, x, y) + pltpu.roll(jnp.where(m, y, x), 4, 0)
        return jnp.where(m, x + pltpu.roll(x, 8 - h, 0), y + pltpu.roll(y, h, 0))

    def power_body(g, carry):
        level = []
        for i in (0, 4, 2, 6, 1, 5, 3, 7):
            x = f_ref[g * 8 + i]
            level.append(x * x)
        for h in (4, 2, 1):
            level = [combine(level[2 * j], level[2 * j + 1], h) for j in range(len(level) // 2)]
        start = pl.multiple_of(n_pair + g * 8, 8)
        rows_ref[pl.ds(start, 8), :] = level[0]
        return carry

    lax.fori_loop(0, n_date // 8, power_body, 0)

    def pair_body(g, carry):
        level = []
        for i in (0, 4, 2, 6, 1, 5, 3, 7):
            p = g * 8 + i
            level.append(f_ref[pairs_s[p, 0]] * g_ref[pairs_s[p, 1]])
        for h in (4, 2, 1):
            level = [combine(level[2 * j], level[2 * j + 1], h) for j in range(len(level) // 2)]
        start = pl.multiple_of(g * 8, 8)
        rows_ref[pl.ds(start, 8), :] = level[0]
        return carry

    lax.fori_loop(0, n_pair // 8, pair_body, 0)

    looked = dot3(split3(rows_ref[...]), window_ref[...], True)
    looked_cross = looked[0:n_pair]
    looked_pow = looked[n_pair:n_pair + n_date]

    date_idx = lax.broadcasted_iota(jnp.int32, (n_pair, n_date), 1)
    sel_a = (pairs_v[:, 0:1] == date_idx).astype(jnp.bfloat16)
    sel_b = (pairs_v[:, 1:2] == date_idx).astype(jnp.bfloat16)
    pow_parts = split3(looked_pow)
    looked_ref = dot3(pow_parts, sel_a, False)
    looked_sec = dot3(pow_parts, sel_b, False)

    proxy = looked_cross / jnp.sqrt(looked_ref * looked_sec + 1e-06)
    series = dot3(split3(proxy), inv_ref[...], False)
    for s in range(series.shape[0]):
        out_ref[s] = series[s:s + 1, :]


def regroup_kernel(in_hbm, out_ref, in_ref, sems):
    n_chunk = out_ref.shape[0]
    half = n_chunk // 2
    rows_half = half * LOOK_R
    copies = []
    for k in range(2):
        for q in range(2):
            rows = pl.ds(q * rows_half, rows_half)
            copy = pltpu.make_async_copy(in_hbm.at[k, rows], in_ref.at[k, rows], sems.at[2 * k + q])
            copy.start()
            copies.append(copy)
    for k in range(2):
        for q in range(2):
            copies[2 * k + q].wait()
            for c in range(q * half, (q + 1) * half):
                out_ref[c, k * LOOK_R:(k + 1) * LOOK_R, :] = in_ref[k, c * LOOK_R:(c + 1) * LOOK_R, :]


def per_device(slc, pairs, inverse):
    n_date = lax.axis_size("date")
    n_pair = pairs.shape[0]
    steps = inverse.shape[0]
    _, _, all_rows, cols = slc.shape
    rows = all_rows // n_date
    chunks = pl.pallas_call(
        regroup_kernel,
        out_shape=jax.ShapeDtypeStruct((n_date, 2 * rows, cols), slc.dtype),
        in_specs=[pl.BlockSpec(memory_space=pl.ANY)],
        out_specs=pl.BlockSpec(memory_space=pltpu.VMEM),
        scratch_shapes=[pltpu.VMEM(slc.shape[1:], slc.dtype), pltpu.SemaphoreType.DMA((4,))],
    )(slc[0])
    stripes = lax.all_to_all(chunks, "date", split_axis=0, concat_axis=0, tiled=True)
    assert rows == LOOK_R and n_date % 8 == 0 and n_pair % 8 == 0
    looks = cols // LOOK_C
    col = lax.broadcasted_iota(jnp.int32, (cols, looks), 0) // LOOK_C
    window = (col == lax.broadcasted_iota(jnp.int32, (cols, looks), 1)).astype(jnp.bfloat16)
    out = pl.pallas_call(
        functools.partial(kernel, n_date, n_pair),
        out_shape=jax.ShapeDtypeStruct((steps, 1, looks), jnp.float32),
        in_specs=[
            pl.BlockSpec(memory_space=pltpu.SMEM),
            pl.BlockSpec(memory_space=pltpu.VMEM),
            pl.BlockSpec(memory_space=pltpu.VMEM),
            pl.BlockSpec(memory_space=pltpu.VMEM),
            pl.BlockSpec(memory_space=pltpu.VMEM),
        ],
        out_specs=pl.BlockSpec(memory_space=pltpu.VMEM),
        scratch_shapes=[
            pltpu.VMEM((n_date, 2 * LOOK_R, cols), jnp.float32),
            pltpu.VMEM((n_date, 2 * LOOK_R, cols), jnp.float32),
            pltpu.VMEM((n_pair + n_date, cols), jnp.float32),
        ],
        compiler_params=pltpu.CompilerParams(vmem_limit_bytes=24 * 1024 * 1024),
    )(pairs, pairs, stripes, inverse, window)
    return out


def solution(mesh):
    in_specs = (P("date", None, "grp", None), P(), P())
    out_specs = P(None, ("grp", "date"), None)
    return jax.shard_map(
        per_device, mesh=mesh, in_specs=in_specs, out_specs=out_specs, check_vma=False
    )
```

```python
import functools

import jax
import jax.numpy as jnp
from jax import lax
from jax.experimental import pallas as pl
from jax.experimental.pallas import tpu as pltpu
from jax.sharding import PartitionSpec as P

LOOK_R = 4
LOOK_C = 16


def split3(x):
    hi = x.astype(jnp.bfloat16)
    rest = x - hi.astype(jnp.float32)
    mid = rest.astype(jnp.bfloat16)
    lo = (rest - mid.astype(jnp.float32)).astype(jnp.bfloat16)
    return hi, mid, lo


def dot3(parts, w, lhs_is_split):
    out = None
    for part in parts:
        if lhs_is_split:
            term = jnp.dot(part, w, preferred_element_type=jnp.float32)
        else:
            term = jnp.dot(w, part, preferred_element_type=jnp.float32)
        out = term if out is None else out + term
    return out


def kernel(n_date, n_pair, pairs_s, pairs_v, st_ref, inv_ref, window_ref, out_ref, f_ref, g_ref, rows_ref, lp_ref, proxy_ref):
    cols = st_ref.shape[-1]
    looks = cols // LOOK_C

    sub = lax.broadcasted_iota(jnp.int32, (2 * LOOK_R, cols), 0)
    sign = jnp.where(sub < LOOK_R, -1.0, 1.0).astype(jnp.float32)

    def date_body(d, carry):
        x = st_ref[d].astype(jnp.float32)
        f_ref[d] = x
        g_ref[d] = pltpu.roll(x, LOOK_R, 0) * sign
        return carry

    lax.fori_loop(0, n_date, date_body, 0)

    masks = {h: (sub & h) == 0 for h in (4, 2, 1)}

    def combine(x, y, h):
        m = masks[h]
        if h == 4:
            return jnp.where(m, x, y) + pltpu.roll(jnp.where(m, y, x), 4, 0)
        return jnp.where(m, x + pltpu.roll(x, 8 - h, 0), y + pltpu.roll(y, h, 0))

    def power_body(g, carry):
        level = []
        for i in (0, 4, 2, 6, 1, 5, 3, 7):
            x = f_ref[g * 8 + i]
            level.append(x * x)
        for h in (4, 2, 1):
            level = [combine(level[2 * j], level[2 * j + 1], h) for j in range(len(level) // 2)]
        start = pl.multiple_of(n_pair + g * 8, 8)
        rows_ref[pl.ds(start, 8), :] = level[0]
        return carry

    lax.fori_loop(0, n_date // 8, power_body, 0)

    def pair_body(g, carry):
        level = []
        for i in (0, 4, 2, 6, 1, 5, 3, 7):
            p = g * 8 + i
            level.append(f_ref[pairs_s[p, 0]] * g_ref[pairs_s[p, 1]])
        for h in (4, 2, 1):
            level = [combine(level[2 * j], level[2 * j + 1], h) for j in range(len(level) // 2)]
        start = pl.multiple_of(g * 8, 8)
        rows_ref[pl.ds(start, 8), :] = level[0]
        return carry

    lax.fori_loop(0, n_pair // 8, pair_body, 0)

    looked = dot3(split3(rows_ref[...]), window_ref[...], True)
    looked_pow = looked[n_pair:n_pair + n_date]
    rows_ref[0:n_pair, 0:looks] = looked[0:n_pair]

    for d in range(n_date):
        lp_ref[d] = jnp.broadcast_to(looked_pow[d:d + 1, :], (8, looks))
    lp_sub = lax.broadcasted_iota(jnp.int32, (8, looks), 0)

    def proxy_body(g, carry):
        ref_pow = jnp.zeros((8, looks), jnp.float32)
        sec_pow = jnp.zeros((8, looks), jnp.float32)
        for i in range(8):
            p = g * 8 + i
            ref_pow = jnp.where(lp_sub == i, lp_ref[pairs_s[p, 0]], ref_pow)
            sec_pow = jnp.where(lp_sub == i, lp_ref[pairs_s[p, 1]], sec_pow)
        start = pl.multiple_of(g * 8, 8)
        cross = rows_ref[pl.ds(start, 8), 0:looks]
        proxy_ref[pl.ds(start, 8), :] = cross / jnp.sqrt(ref_pow * sec_pow + 1e-06)
        return carry

    lax.fori_loop(0, n_pair // 8, proxy_body, 0)
    proxy = proxy_ref[...]
    series = dot3(split3(proxy), inv_ref[...], False)
    for s in range(series.shape[0]):
        out_ref[s] = series[s:s + 1, :]


def regroup_kernel(in_hbm, out_ref, in_ref, sems):
    n_chunk = out_ref.shape[0]
    half = n_chunk // 2
    rows_half = half * LOOK_R
    copies = []
    for k in range(2):
        for q in range(2):
            rows = pl.ds(q * rows_half, rows_half)
            copy = pltpu.make_async_copy(in_hbm.at[k, rows], in_ref.at[k, rows], sems.at[2 * k + q])
            copy.start()
            copies.append(copy)
    for k in range(2):
        for q in range(2):
            copies[2 * k + q].wait()
            for c in range(q * half, (q + 1) * half):
                out_ref[c, k * LOOK_R:(k + 1) * LOOK_R, :] = in_ref[k, c * LOOK_R:(c + 1) * LOOK_R, :]


def per_device(slc, pairs, inverse):
    n_date = lax.axis_size("date")
    n_pair = pairs.shape[0]
    steps = inverse.shape[0]
    _, _, all_rows, cols = slc.shape
    rows = all_rows // n_date
    chunks = pl.pallas_call(
        regroup_kernel,
        out_shape=jax.ShapeDtypeStruct((n_date, 2 * rows, cols), slc.dtype),
        in_specs=[pl.BlockSpec(memory_space=pl.ANY)],
        out_specs=pl.BlockSpec(memory_space=pltpu.VMEM),
        scratch_shapes=[pltpu.VMEM(slc.shape[1:], slc.dtype), pltpu.SemaphoreType.DMA((4,))],
    )(slc[0])
    stripes = lax.all_to_all(chunks, "date", split_axis=0, concat_axis=0, tiled=True)
    assert rows == LOOK_R and n_date % 8 == 0 and n_pair % 8 == 0
    looks = cols // LOOK_C
    col = lax.broadcasted_iota(jnp.int32, (cols, looks), 0) // LOOK_C
    window = (col == lax.broadcasted_iota(jnp.int32, (cols, looks), 1)).astype(jnp.bfloat16)
    out = pl.pallas_call(
        functools.partial(kernel, n_date, n_pair),
        out_shape=jax.ShapeDtypeStruct((steps, 1, looks), jnp.float32),
        in_specs=[
            pl.BlockSpec(memory_space=pltpu.SMEM),
            pl.BlockSpec(memory_space=pltpu.VMEM),
            pl.BlockSpec(memory_space=pltpu.VMEM),
            pl.BlockSpec(memory_space=pltpu.VMEM),
            pl.BlockSpec(memory_space=pltpu.VMEM),
        ],
        out_specs=pl.BlockSpec(memory_space=pltpu.VMEM),
        scratch_shapes=[
            pltpu.VMEM((n_date, 2 * LOOK_R, cols), jnp.float32),
            pltpu.VMEM((n_date, 2 * LOOK_R, cols), jnp.float32),
            pltpu.VMEM((n_pair + n_date, cols), jnp.float32),
            pltpu.VMEM((n_date, 8, looks), jnp.float32),
            pltpu.VMEM((n_pair, looks), jnp.float32),
        ],
        compiler_params=pltpu.CompilerParams(vmem_limit_bytes=24 * 1024 * 1024),
    )(pairs, pairs, stripes, inverse, window)
    return out


def solution(mesh):
    in_specs = (P("date", None, "grp", None), P(), P())
    out_specs = P(None, ("grp", "date"), None)
    return jax.shard_map(
        per_device, mesh=mesh, in_specs=in_specs, out_specs=out_specs, check_vma=False
    )
```

```python
import functools

import jax
import jax.numpy as jnp
from jax import lax
from jax.experimental import pallas as pl
from jax.experimental.pallas import tpu as pltpu
from jax.sharding import PartitionSpec as P

LOOK_R = 4
LOOK_C = 16


def split3(x):
    hi = x.astype(jnp.bfloat16)
    rest = x - hi.astype(jnp.float32)
    mid = rest.astype(jnp.bfloat16)
    lo = (rest - mid.astype(jnp.float32)).astype(jnp.bfloat16)
    return hi, mid, lo


def dot3(parts, w, lhs_is_split):
    out = None
    for part in parts:
        if lhs_is_split:
            term = jnp.dot(part, w, preferred_element_type=jnp.float32)
        else:
            term = jnp.dot(w, part, preferred_element_type=jnp.float32)
        out = term if out is None else out + term
    return out


def kernel(n_date, n_pair, pairs_any, pairs_v, st_ref, inv_ref, window_ref, out_ref, f_ref, g_ref, rows_ref,
           pairs_s, pairs_sem):
    pairs_copy = pltpu.make_async_copy(pairs_any, pairs_s, pairs_sem)
    pairs_copy.start()
    cols = st_ref.shape[-1]
    looks = cols // LOOK_C

    sub = lax.broadcasted_iota(jnp.int32, (2 * LOOK_R, cols), 0)
    sign = jnp.where(sub < LOOK_R, -1.0, 1.0).astype(jnp.float32)

    def date_body(d, carry):
        x = st_ref[d].astype(jnp.float32)
        f_ref[d] = x
        g_ref[d] = pltpu.roll(x, LOOK_R, 0) * sign
        return carry

    lax.fori_loop(0, n_date, date_body, 0)

    masks = {h: (sub & h) == 0 for h in (4, 2, 1)}

    def combine(x, y, h):
        m = masks[h]
        if h == 4:
            return jnp.where(m, x, y) + pltpu.roll(jnp.where(m, y, x), 4, 0)
        return jnp.where(m, x + pltpu.roll(x, 8 - h, 0), y + pltpu.roll(y, h, 0))

    def power_body(g, carry):
        level = []
        for i in (0, 4, 2, 6, 1, 5, 3, 7):
            x = f_ref[g * 8 + i]
            level.append(x * x)
        for h in (4, 2, 1):
            level = [combine(level[2 * j], level[2 * j + 1], h) for j in range(len(level) // 2)]
        start = pl.multiple_of(n_pair + g * 8, 8)
        rows_ref[pl.ds(start, 8), :] = level[0]
        return carry

    lax.fori_loop(0, n_date // 8, power_body, 0)

    pairs_copy.wait()

    def pair_body(g, carry):
        level = []
        for i in (0, 4, 2, 6, 1, 5, 3, 7):
            p = g * 8 + i
            level.append(f_ref[pairs_s[p, 0]] * g_ref[pairs_s[p, 1]])
        for h in (4, 2, 1):
            level = [combine(level[2 * j], level[2 * j + 1], h) for j in range(len(level) // 2)]
        start = pl.multiple_of(g * 8, 8)
        rows_ref[pl.ds(start, 8), :] = level[0]
        return carry

    lax.fori_loop(0, n_pair // 8, pair_body, 0)

    looked = dot3(split3(rows_ref[...]), window_ref[...], True)
    looked_cross = looked[0:n_pair]
    looked_pow = looked[n_pair:n_pair + n_date]

    date_idx = lax.broadcasted_iota(jnp.int32, (n_pair, n_date), 1)
    sel_a = (pairs_v[:, 0:1] == date_idx).astype(jnp.bfloat16)
    sel_b = (pairs_v[:, 1:2] == date_idx).astype(jnp.bfloat16)
    pow_parts = split3(looked_pow)
    looked_ref = dot3(pow_parts, sel_a, False)
    looked_sec = dot3(pow_parts, sel_b, False)

    proxy = looked_cross / jnp.sqrt(looked_ref * looked_sec + 1e-06)
    series = dot3(split3(proxy), inv_ref[...], False)
    for s in range(series.shape[0]):
        out_ref[s] = series[s:s + 1, :]


def regroup_kernel(in_hbm, out_ref, in_ref, sems):
    n_chunk = out_ref.shape[0]
    half = n_chunk // 2
    rows_half = half * LOOK_R
    copies = []
    for k in range(2):
        for q in range(2):
            rows = pl.ds(q * rows_half, rows_half)
            copy = pltpu.make_async_copy(in_hbm.at[k, rows], in_ref.at[k, rows], sems.at[2 * k + q])
            copy.start()
            copies.append(copy)
    for k in range(2):
        for q in range(2):
            copies[2 * k + q].wait()
            for c in range(q * half, (q + 1) * half):
                out_ref[c, k * LOOK_R:(k + 1) * LOOK_R, :] = in_ref[k, c * LOOK_R:(c + 1) * LOOK_R, :]


def per_device(slc, pairs, inverse):
    n_date = lax.axis_size("date")
    n_pair = pairs.shape[0]
    steps = inverse.shape[0]
    _, _, all_rows, cols = slc.shape
    rows = all_rows // n_date
    chunks = pl.pallas_call(
        regroup_kernel,
        out_shape=jax.ShapeDtypeStruct((n_date, 2 * rows, cols), slc.dtype),
        in_specs=[pl.BlockSpec(memory_space=pl.ANY)],
        out_specs=pl.BlockSpec(memory_space=pltpu.VMEM),
        scratch_shapes=[pltpu.VMEM(slc.shape[1:], slc.dtype), pltpu.SemaphoreType.DMA((4,))],
    )(slc[0])
    stripes = lax.all_to_all(chunks, "date", split_axis=0, concat_axis=0, tiled=True)
    assert rows == LOOK_R and n_date % 8 == 0 and n_pair % 8 == 0
    looks = cols // LOOK_C
    col = lax.broadcasted_iota(jnp.int32, (cols, looks), 0) // LOOK_C
    window = (col == lax.broadcasted_iota(jnp.int32, (cols, looks), 1)).astype(jnp.bfloat16)
    out = pl.pallas_call(
        functools.partial(kernel, n_date, n_pair),
        out_shape=jax.ShapeDtypeStruct((steps, 1, looks), jnp.float32),
        in_specs=[
            pl.BlockSpec(memory_space=pl.ANY),
            pl.BlockSpec(memory_space=pltpu.VMEM),
            pl.BlockSpec(memory_space=pltpu.VMEM),
            pl.BlockSpec(memory_space=pltpu.VMEM),
            pl.BlockSpec(memory_space=pltpu.VMEM),
        ],
        out_specs=pl.BlockSpec(memory_space=pltpu.VMEM),
        scratch_shapes=[
            pltpu.VMEM((n_date, 2 * LOOK_R, cols), jnp.float32),
            pltpu.VMEM((n_date, 2 * LOOK_R, cols), jnp.float32),
            pltpu.VMEM((n_pair + n_date, cols), jnp.float32),
            pltpu.SMEM(pairs.shape, pairs.dtype),
            pltpu.SemaphoreType.DMA(()),
        ],
        compiler_params=pltpu.CompilerParams(vmem_limit_bytes=24 * 1024 * 1024),
    )(pairs, pairs, stripes, inverse, window)
    return out


def solution(mesh):
    in_specs = (P("date", None, "grp", None), P(), P())
    out_specs = P(None, ("grp", "date"), None)
    return jax.shard_map(
        per_device, mesh=mesh, in_specs=in_specs, out_specs=out_specs, check_vma=False
    )
```

```python
import functools

import jax
import jax.numpy as jnp
from jax import lax
from jax.experimental import pallas as pl
from jax.experimental.pallas import tpu as pltpu
from jax.sharding import PartitionSpec as P

LOOK_R = 4
LOOK_C = 16


def split3(x):
    hi = x.astype(jnp.bfloat16)
    rest = x - hi.astype(jnp.float32)
    mid = rest.astype(jnp.bfloat16)
    lo = (rest - mid.astype(jnp.float32)).astype(jnp.bfloat16)
    return hi, mid, lo


def dot3(parts, w, lhs_is_split):
    out = None
    for part in parts:
        if lhs_is_split:
            term = jnp.dot(part, w, preferred_element_type=jnp.float32)
        else:
            term = jnp.dot(w, part, preferred_element_type=jnp.float32)
        out = term if out is None else out + term
    return out


def kernel(n_date, n_pair, pairs_any, pairs_v, st_ref, inv_ref, window_ref, out_ref, f_ref, g_ref, rows_ref,
           pairs_s, pairs_sem):
    pairs_copy = pltpu.make_async_copy(pairs_any, pairs_s, pairs_sem)
    pairs_copy.start()
    cols = st_ref.shape[-1]
    looks = cols // LOOK_C

    sub = lax.broadcasted_iota(jnp.int32, (2 * LOOK_R, cols), 0)
    sign = jnp.where(sub < LOOK_R, -1.0, 1.0).astype(jnp.float32)

    def date_body(d, carry):
        x = st_ref[d].astype(jnp.float32)
        f_ref[d] = x
        g_ref[d] = pltpu.roll(x, LOOK_R, 0) * sign
        return carry

    lax.fori_loop(0, n_date, date_body, 0)

    masks = {h: (sub & h) == 0 for h in (4, 2, 1)}

    def combine(x, y, h):
        m = masks[h]
        if h == 4:
            return jnp.where(m, x, y) + pltpu.roll(jnp.where(m, y, x), 4, 0)
        return jnp.where(m, x + pltpu.roll(x, 8 - h, 0), y + pltpu.roll(y, h, 0))

    def power_body(g, carry):
        level = []
        for i in (0, 4, 2, 6, 1, 5, 3, 7):
            x = f_ref[g * 8 + i]
            level.append(x * x)
        for h in (4, 2, 1):
            level = [combine(level[2 * j], level[2 * j + 1], h) for j in range(len(level) // 2)]
        start = pl.multiple_of(n_pair + g * 8, 8)
        rows_ref[pl.ds(start, 8), :] = level[0]
        return carry

    lax.fori_loop(0, n_date // 8, power_body, 0)

    pairs_copy.wait()

    def pair_body(g, carry):
        level = []
        for i in (0, 4, 2, 6, 1, 5, 3, 7):
            p = g * 8 + i
            level.append(f_ref[pairs_s[p, 0]] * g_ref[pairs_s[p, 1]])
        for h in (4, 2, 1):
            level = [combine(level[2 * j], level[2 * j + 1], h) for j in range(len(level) // 2)]
        start = pl.multiple_of(g * 8, 8)
        rows_ref[pl.ds(start, 8), :] = level[0]
        return carry

    lax.fori_loop(0, n_pair // 8, pair_body, 0)

    n_rows = n_pair + n_date
    stacked = jnp.concatenate(split3(rows_ref[...]), axis=0)
    parts = jnp.dot(stacked, window_ref[...], preferred_element_type=jnp.float32)
    looked = (parts[0:n_rows] + parts[n_rows:2 * n_rows]) + parts[2 * n_rows:3 * n_rows]
    looked_cross = looked[0:n_pair]
    looked_pow = looked[n_pair:n_pair + n_date]

    date_idx = lax.broadcasted_iota(jnp.int32, (n_pair, n_date), 1)
    sel_a = (pairs_v[:, 0:1] == date_idx).astype(jnp.bfloat16)
    sel_b = (pairs_v[:, 1:2] == date_idx).astype(jnp.bfloat16)
    picked = dot3(split3(looked_pow), jnp.concatenate([sel_a, sel_b], axis=0), False)
    looked_ref = picked[0:n_pair]
    looked_sec = picked[n_pair:2 * n_pair]

    proxy = looked_cross / jnp.sqrt(looked_ref * looked_sec + 1e-06)
    series = dot3(split3(proxy), inv_ref[...], False)
    for s in range(series.shape[0]):
        out_ref[s] = series[s:s + 1, :]


def regroup_kernel(in_hbm, out_ref, in_ref, sems):
    n_chunk = out_ref.shape[0]
    half = n_chunk // 2
    rows_half = half * LOOK_R
    copies = []
    for k in range(2):
        for q in range(2):
            rows = pl.ds(q * rows_half, rows_half)
            copy = pltpu.make_async_copy(in_hbm.at[k, rows], in_ref.at[k, rows], sems.at[2 * k + q])
            copy.start()
            copies.append(copy)
    for k in range(2):
        for q in range(2):
            copies[2 * k + q].wait()
            for c in range(q * half, (q + 1) * half):
                out_ref[c, k * LOOK_R:(k + 1) * LOOK_R, :] = in_ref[k, c * LOOK_R:(c + 1) * LOOK_R, :]


def per_device(slc, pairs, inverse):
    n_date = lax.axis_size("date")
    n_pair = pairs.shape[0]
    steps = inverse.shape[0]
    _, _, all_rows, cols = slc.shape
    rows = all_rows // n_date
    chunks = pl.pallas_call(
        regroup_kernel,
        out_shape=jax.ShapeDtypeStruct((n_date, 2 * rows, cols), slc.dtype),
        in_specs=[pl.BlockSpec(memory_space=pl.ANY)],
        out_specs=pl.BlockSpec(memory_space=pltpu.VMEM),
        scratch_shapes=[pltpu.VMEM(slc.shape[1:], slc.dtype), pltpu.SemaphoreType.DMA((4,))],
    )(slc[0])
    stripes = lax.all_to_all(chunks, "date", split_axis=0, concat_axis=0, tiled=True)
    assert rows == LOOK_R and n_date % 8 == 0 and n_pair % 8 == 0
    looks = cols // LOOK_C
    col = lax.broadcasted_iota(jnp.int32, (cols, looks), 0) // LOOK_C
    window = (col == lax.broadcasted_iota(jnp.int32, (cols, looks), 1)).astype(jnp.bfloat16)
    out = pl.pallas_call(
        functools.partial(kernel, n_date, n_pair),
        out_shape=jax.ShapeDtypeStruct((steps, 1, looks), jnp.float32),
        in_specs=[
            pl.BlockSpec(memory_space=pl.ANY),
            pl.BlockSpec(memory_space=pltpu.VMEM),
            pl.BlockSpec(memory_space=pltpu.VMEM),
            pl.BlockSpec(memory_space=pltpu.VMEM),
            pl.BlockSpec(memory_space=pltpu.VMEM),
        ],
        out_specs=pl.BlockSpec(memory_space=pltpu.VMEM),
        scratch_shapes=[
            pltpu.VMEM((n_date, 2 * LOOK_R, cols), jnp.float32),
            pltpu.VMEM((n_date, 2 * LOOK_R, cols), jnp.float32),
            pltpu.VMEM((n_pair + n_date, cols), jnp.float32),
            pltpu.SMEM(pairs.shape, pairs.dtype),
            pltpu.SemaphoreType.DMA(()),
        ],
        compiler_params=pltpu.CompilerParams(vmem_limit_bytes=24 * 1024 * 1024),
    )(pairs, pairs, stripes, inverse, window)
    return out


def solution(mesh):
    in_specs = (P("date", None, "grp", None), P(), P())
    out_specs = P(None, ("grp", "date"), None)
    return jax.shard_map(
        per_device, mesh=mesh, in_specs=in_specs, out_specs=out_specs, check_vma=False
    )
```

```python
import functools

import jax
import jax.numpy as jnp
from jax import lax
from jax.experimental import pallas as pl
from jax.experimental.pallas import tpu as pltpu
from jax.sharding import PartitionSpec as P

LOOK_R = 4
LOOK_C = 16


def split3(x):
    hi = x.astype(jnp.bfloat16)
    rest = x - hi.astype(jnp.float32)
    mid = rest.astype(jnp.bfloat16)
    lo = (rest - mid.astype(jnp.float32)).astype(jnp.bfloat16)
    return hi, mid, lo


def dot3(parts, w, lhs_is_split):
    out = None
    for part in parts:
        if lhs_is_split:
            term = jnp.dot(part, w, preferred_element_type=jnp.float32)
        else:
            term = jnp.dot(w, part, preferred_element_type=jnp.float32)
        out = term if out is None else out + term
    return out


def kernel(n_date, n_pair, pairs_any, pairs_v, st_ref, inv_ref, window_ref, out_ref, f_ref, g_ref, rows_ref,
           pairs_s, pairs_sem):
    pairs_copy = pltpu.make_async_copy(pairs_any, pairs_s, pairs_sem)
    pairs_copy.start()
    cols = st_ref.shape[-1]
    looks = cols // LOOK_C

    sub = lax.broadcasted_iota(jnp.int32, (2 * LOOK_R, cols), 0)
    sign = jnp.where(sub < LOOK_R, -1.0, 1.0).astype(jnp.float32)

    def date_body(d, carry):
        x = st_ref[d].astype(jnp.float32)
        f_ref[d] = x
        g_ref[d] = pltpu.roll(x, LOOK_R, 0) * sign
        return carry

    lax.fori_loop(0, n_date, date_body, 0)

    masks = {h: (sub & h) == 0 for h in (4, 2, 1)}

    def combine(x, y, h):
        m = masks[h]
        if h == 4:
            return jnp.where(m, x, y) + pltpu.roll(jnp.where(m, y, x), 4, 0)
        return jnp.where(m, x + pltpu.roll(x, 8 - h, 0), y + pltpu.roll(y, h, 0))

    def power_body(g, carry):
        level = []
        for i in (0, 4, 2, 6, 1, 5, 3, 7):
            x = f_ref[g * 8 + i]
            level.append(x * x)
        for h in (4, 2, 1):
            level = [combine(level[2 * j], level[2 * j + 1], h) for j in range(len(level) // 2)]
        start = pl.multiple_of(n_pair + g * 8, 8)
        rows_ref[pl.ds(start, 8), :] = level[0]
        return carry

    lax.fori_loop(0, n_date // 8, power_body, 0)

    pairs_copy.wait()

    def pair_body(g, carry):
        level = []
        for i in (0, 4, 2, 6, 1, 5, 3, 7):
            p = g * 8 + i
            level.append(f_ref[pairs_s[p, 0]] * g_ref[pairs_s[p, 1]])
        for h in (4, 2, 1):
            level = [combine(level[2 * j], level[2 * j + 1], h) for j in range(len(level) // 2)]
        start = pl.multiple_of(g * 8, 8)
        rows_ref[pl.ds(start, 8), :] = level[0]
        return carry

    lax.fori_loop(0, n_pair // 8, pair_body, 0)

    n_rows = n_pair + n_date
    stacked = jnp.concatenate(split3(rows_ref[...]), axis=0)
    parts = jnp.dot(stacked, window_ref[...], preferred_element_type=jnp.float32)
    looked = (parts[0:n_rows] + parts[n_rows:2 * n_rows]) + parts[2 * n_rows:3 * n_rows]
    looked_cross = looked[0:n_pair]
    looked_pow = looked[n_pair:n_pair + n_date]

    date_idx = lax.broadcasted_iota(jnp.int32, (n_pair, n_date), 1)
    sel_a = (pairs_v[:, 0:1] == date_idx).astype(jnp.bfloat16)
    sel_b = (pairs_v[:, 1:2] == date_idx).astype(jnp.bfloat16)
    picked = dot3(split3(looked_pow), jnp.concatenate([sel_a, sel_b], axis=0), False)
    looked_ref = picked[0:n_pair]
    looked_sec = picked[n_pair:2 * n_pair]

    proxy = looked_cross / jnp.sqrt(looked_ref * looked_sec + 1e-06)
    series = dot3(split3(proxy), inv_ref[...], False)
    for s in range(series.shape[0]):
        out_ref[s] = series[s:s + 1, :]


def regroup_kernel(in_hbm, out_hbm, in_ref, sems, out_sems):
    n_chunk = out_hbm.shape[0]
    half = n_chunk // 2
    rows_half = half * LOOK_R
    copies = []
    for k in range(2):
        for q in range(2):
            rows = pl.ds(q * rows_half, rows_half)
            copy = pltpu.make_async_copy(in_hbm.at[k, rows], in_ref.at[k, rows], sems.at[2 * k + q])
            copy.start()
            copies.append(copy)
    outs = []
    for k in range(2):
        for q in range(2):
            copies[2 * k + q].wait()
            for c in range(q * half, (q + 1) * half):
                out = pltpu.make_async_copy(
                    in_ref.at[k, pl.ds(c * LOOK_R, LOOK_R)],
                    out_hbm.at[c, pl.ds(k * LOOK_R, LOOK_R)],
                    out_sems.at[k * n_chunk + c],
                )
                out.start()
                outs.append(out)
    for out in outs:
        out.wait()


def per_device(slc, pairs, inverse):
    n_date = lax.axis_size("date")
    n_pair = pairs.shape[0]
    steps = inverse.shape[0]
    _, _, all_rows, cols = slc.shape
    rows = all_rows // n_date
    chunks = pl.pallas_call(
        regroup_kernel,
        out_shape=jax.ShapeDtypeStruct((n_date, 2 * rows, cols), slc.dtype),
        in_specs=[pl.BlockSpec(memory_space=pl.ANY)],
        out_specs=pl.BlockSpec(memory_space=pl.ANY),
        scratch_shapes=[
            pltpu.VMEM(slc.shape[1:], slc.dtype),
            pltpu.SemaphoreType.DMA((4,)),
            pltpu.SemaphoreType.DMA((2 * n_date,)),
        ],
    )(slc[0])
    stripes = lax.all_to_all(chunks, "date", split_axis=0, concat_axis=0, tiled=True)
    assert rows == LOOK_R and n_date % 8 == 0 and n_pair % 8 == 0
    looks = cols // LOOK_C
    col = lax.broadcasted_iota(jnp.int32, (cols, looks), 0) // LOOK_C
    window = (col == lax.broadcasted_iota(jnp.int32, (cols, looks), 1)).astype(jnp.bfloat16)
    out = pl.pallas_call(
        functools.partial(kernel, n_date, n_pair),
        out_shape=jax.ShapeDtypeStruct((steps, 1, looks), jnp.float32),
        in_specs=[
            pl.BlockSpec(memory_space=pl.ANY),
            pl.BlockSpec(memory_space=pltpu.VMEM),
            pl.BlockSpec(memory_space=pltpu.VMEM),
            pl.BlockSpec(memory_space=pltpu.VMEM),
            pl.BlockSpec(memory_space=pltpu.VMEM),
        ],
        out_specs=pl.BlockSpec(memory_space=pltpu.VMEM),
        scratch_shapes=[
            pltpu.VMEM((n_date, 2 * LOOK_R, cols), jnp.float32),
            pltpu.VMEM((n_date, 2 * LOOK_R, cols), jnp.float32),
            pltpu.VMEM((n_pair + n_date, cols), jnp.float32),
            pltpu.SMEM(pairs.shape, pairs.dtype),
            pltpu.SemaphoreType.DMA(()),
        ],
        compiler_params=pltpu.CompilerParams(vmem_limit_bytes=24 * 1024 * 1024),
    )(pairs, pairs, stripes, inverse, window)
    return out


def solution(mesh):
    in_specs = (P("date", None, "grp", None), P(), P())
    out_specs = P(None, ("grp", "date"), None)
    return jax.shard_map(
        per_device, mesh=mesh, in_specs=in_specs, out_specs=out_specs, check_vma=False
    )
```

```python
import functools

import jax
import jax.numpy as jnp
from jax import lax
from jax.experimental import pallas as pl
from jax.experimental.pallas import tpu as pltpu
from jax.sharding import PartitionSpec as P

LOOK_R = 4
LOOK_C = 16


def split3(x):
    hi = x.astype(jnp.bfloat16)
    rest = x - hi.astype(jnp.float32)
    mid = rest.astype(jnp.bfloat16)
    lo = (rest - mid.astype(jnp.float32)).astype(jnp.bfloat16)
    return hi, mid, lo


def dot3(parts, w, lhs_is_split):
    out = None
    for part in parts:
        if lhs_is_split:
            term = jnp.dot(part, w, preferred_element_type=jnp.float32)
        else:
            term = jnp.dot(w, part, preferred_element_type=jnp.float32)
        out = term if out is None else out + term
    return out


def kernel(n_date, n_pair, pairs_any, pairs_v, st_ref, inv_ref, window_ref, out_ref, f_ref, g_ref, rows_ref,
           pairs_s, pairs_sem):
    pairs_copy = pltpu.make_async_copy(pairs_any, pairs_s, pairs_sem)
    pairs_copy.start()
    cols = st_ref.shape[-1]
    looks = cols // LOOK_C

    sub = lax.broadcasted_iota(jnp.int32, (2 * LOOK_R, cols), 0)
    sign = jnp.where(sub < LOOK_R, -1.0, 1.0).astype(jnp.float32)

    def date_body(d, carry):
        x = st_ref[d].astype(jnp.float32)
        f_ref[d] = x
        g_ref[d] = pltpu.roll(x, LOOK_R, 0) * sign
        return carry

    lax.fori_loop(0, n_date, date_body, 0)

    masks = {h: (sub & h) == 0 for h in (4, 2, 1)}

    def combine(x, y, h):
        m = masks[h]
        if h == 4:
            return jnp.where(m, x, y) + pltpu.roll(jnp.where(m, y, x), 4, 0)
        return jnp.where(m, x + pltpu.roll(x, 8 - h, 0), y + pltpu.roll(y, h, 0))

    def power_body(g, carry):
        level = []
        for i in (0, 4, 2, 6, 1, 5, 3, 7):
            x = f_ref[g * 8 + i]
            level.append(x * x)
        for h in (4, 2, 1):
            level = [combine(level[2 * j], level[2 * j + 1], h) for j in range(len(level) // 2)]
        start = pl.multiple_of(n_pair + g * 8, 8)
        rows_ref[pl.ds(start, 8), :] = level[0]
        return carry

    lax.fori_loop(0, n_date // 8, power_body, 0)

    pairs_copy.wait()

    def pair_body(g, carry):
        level = []
        for i in (0, 4, 2, 6, 1, 5, 3, 7):
            p = g * 8 + i
            level.append(f_ref[pairs_s[p, 0]] * g_ref[pairs_s[p, 1]])
        for h in (4, 2, 1):
            level = [combine(level[2 * j], level[2 * j + 1], h) for j in range(len(level) // 2)]
        start = pl.multiple_of(g * 8, 8)
        rows_ref[pl.ds(start, 8), :] = level[0]
        return carry

    lax.fori_loop(0, n_pair // 8, pair_body, 0)

    n_rows = n_pair + n_date
    stacked = jnp.concatenate(split3(rows_ref[...]), axis=0)
    parts = jnp.dot(stacked, window_ref[...], preferred_element_type=jnp.float32)
    looked = (parts[0:n_rows] + parts[n_rows:2 * n_rows]) + parts[2 * n_rows:3 * n_rows]
    looked_cross = looked[0:n_pair]
    looked_pow = looked[n_pair:n_pair + n_date]

    date_idx = lax.broadcasted_iota(jnp.int32, (n_pair, n_date), 1)
    sel_a = (pairs_v[:, 0:1] == date_idx).astype(jnp.bfloat16)
    sel_b = (pairs_v[:, 1:2] == date_idx).astype(jnp.bfloat16)
    picked = dot3(split3(looked_pow), jnp.concatenate([sel_a, sel_b], axis=0), False)
    looked_ref = picked[0:n_pair]
    looked_sec = picked[n_pair:2 * n_pair]

    proxy = looked_cross / jnp.sqrt(looked_ref * looked_sec + 1e-06)
    series = dot3(split3(proxy), inv_ref[...], False)
    for s in range(series.shape[0]):
        out_ref[s] = series[s:s + 1, :]


def regroup_kernel(in_hbm, out_ref, in_ref, sems):
    n_chunk = out_ref.shape[0]
    half = n_chunk // 2
    rows_half = half * LOOK_R
    copies = []
    for k in range(2):
        for q in range(2):
            rows = pl.ds(q * rows_half, rows_half)
            copy = pltpu.make_async_copy(in_hbm.at[k, rows], in_ref.at[k, rows], sems.at[2 * k + q])
            copy.start()
            copies.append(copy)
    for k in range(2):
        for q in range(2):
            copies[2 * k + q].wait()
            for c in range(q * half, (q + 1) * half):
                out_ref[c, k * LOOK_R:(k + 1) * LOOK_R, :] = in_ref[k, c * LOOK_R:(c + 1) * LOOK_R, :]


def per_device(slc, pairs, inverse):
    n_date = lax.axis_size("date")
    n_pair = pairs.shape[0]
    steps = inverse.shape[0]
    _, _, all_rows, cols = slc.shape
    rows = all_rows // n_date
    size = 2 * all_rows
    out_i = lax.broadcasted_iota(jnp.int32, (size, size), 0)
    in_i = lax.broadcasted_iota(jnp.int32, (size, size), 1)
    part = (out_i // rows) % 2
    row = (out_i // (2 * rows)) * rows + out_i % rows
    perm = ((in_i // all_rows == part) & (in_i % all_rows == row)).astype(slc.dtype)
    flat = slc[0].reshape(size, cols)
    chunks = jnp.dot(perm, flat, preferred_element_type=jnp.float32).astype(slc.dtype).reshape(n_date, 2 * rows, cols)
    stripes = lax.all_to_all(chunks, "date", split_axis=0, concat_axis=0, tiled=True)
    assert rows == LOOK_R and n_date % 8 == 0 and n_pair % 8 == 0
    looks = cols // LOOK_C
    col = lax.broadcasted_iota(jnp.int32, (cols, looks), 0) // LOOK_C
    window = (col == lax.broadcasted_iota(jnp.int32, (cols, looks), 1)).astype(jnp.bfloat16)
    out = pl.pallas_call(
        functools.partial(kernel, n_date, n_pair),
        out_shape=jax.ShapeDtypeStruct((steps, 1, looks), jnp.float32),
        in_specs=[
            pl.BlockSpec(memory_space=pl.ANY),
            pl.BlockSpec(memory_space=pltpu.VMEM),
            pl.BlockSpec(memory_space=pltpu.VMEM),
            pl.BlockSpec(memory_space=pltpu.VMEM),
            pl.BlockSpec(memory_space=pltpu.VMEM),
        ],
        out_specs=pl.BlockSpec(memory_space=pltpu.VMEM),
        scratch_shapes=[
            pltpu.VMEM((n_date, 2 * LOOK_R, cols), jnp.float32),
            pltpu.VMEM((n_date, 2 * LOOK_R, cols), jnp.float32),
            pltpu.VMEM((n_pair + n_date, cols), jnp.float32),
            pltpu.SMEM(pairs.shape, pairs.dtype),
            pltpu.SemaphoreType.DMA(()),
        ],
        compiler_params=pltpu.CompilerParams(vmem_limit_bytes=24 * 1024 * 1024),
    )(pairs, pairs, stripes, inverse, window)
    return out


def solution(mesh):
    in_specs = (P("date", None, "grp", None), P(), P())
    out_specs = P(None, ("grp", "date"), None)
    return jax.shard_map(
        per_device, mesh=mesh, in_specs=in_specs, out_specs=out_specs, check_vma=False
    )
```

```python
import functools

import jax
import jax.numpy as jnp
from jax import lax
from jax.experimental import pallas as pl
from jax.experimental.pallas import tpu as pltpu
from jax.sharding import PartitionSpec as P

LOOK_R = 4
LOOK_C = 16


def split3(x):
    hi = x.astype(jnp.bfloat16)
    rest = x - hi.astype(jnp.float32)
    mid = rest.astype(jnp.bfloat16)
    lo = (rest - mid.astype(jnp.float32)).astype(jnp.bfloat16)
    return hi, mid, lo


def dot3(parts, w, lhs_is_split):
    out = None
    for part in parts:
        if lhs_is_split:
            term = jnp.dot(part, w, preferred_element_type=jnp.float32)
        else:
            term = jnp.dot(w, part, preferred_element_type=jnp.float32)
        out = term if out is None else out + term
    return out


def kernel(n_date, n_pair, pairs_any, pairs_v, st_ref, inv_ref, window_ref, out_ref, f_ref, g_ref, rows_ref,
           pairs_s, pairs_sem):
    pairs_copy = pltpu.make_async_copy(pairs_any, pairs_s, pairs_sem)
    pairs_copy.start()
    cols = st_ref.shape[-1]
    looks = cols // LOOK_C

    sub = lax.broadcasted_iota(jnp.int32, (2 * LOOK_R, cols), 0)
    sign = jnp.where(sub < LOOK_R, -1.0, 1.0).astype(jnp.float32)

    def date_body(d, carry):
        x = st_ref[d].astype(jnp.float32)
        f_ref[d] = x
        g_ref[d] = pltpu.roll(x, LOOK_R, 0) * sign
        return carry

    lax.fori_loop(0, n_date, date_body, 0)

    masks = {h: (sub & h) == 0 for h in (4, 2, 1)}

    def combine(x, y, h):
        m = masks[h]
        if h == 4:
            return jnp.where(m, x, y) + pltpu.roll(jnp.where(m, y, x), 4, 0)
        return jnp.where(m, x + pltpu.roll(x, 8 - h, 0), y + pltpu.roll(y, h, 0))

    def power_body(g, carry):
        level = []
        for i in (0, 4, 2, 6, 1, 5, 3, 7):
            x = f_ref[g * 8 + i]
            level.append(x * x)
        for h in (4, 2, 1):
            level = [combine(level[2 * j], level[2 * j + 1], h) for j in range(len(level) // 2)]
        start = pl.multiple_of(n_pair + g * 8, 8)
        rows_ref[pl.ds(start, 8), :] = level[0]
        return carry

    lax.fori_loop(0, n_date // 8, power_body, 0)

    pairs_copy.wait()

    def pair_body(g, carry):
        level = []
        for i in (0, 4, 2, 6, 1, 5, 3, 7):
            p = g * 8 + i
            level.append(f_ref[pairs_s[p, 0]] * g_ref[pairs_s[p, 1]])
        for h in (4, 2, 1):
            level = [combine(level[2 * j], level[2 * j + 1], h) for j in range(len(level) // 2)]
        start = pl.multiple_of(g * 8, 8)
        rows_ref[pl.ds(start, 8), :] = level[0]
        return carry

    lax.fori_loop(0, n_pair // 8, pair_body, 0, unroll=2)

    n_rows = n_pair + n_date
    stacked = jnp.concatenate(split3(rows_ref[...]), axis=0)
    parts = jnp.dot(stacked, window_ref[...], preferred_element_type=jnp.float32)
    looked = (parts[0:n_rows] + parts[n_rows:2 * n_rows]) + parts[2 * n_rows:3 * n_rows]
    looked_cross = looked[0:n_pair]
    looked_pow = looked[n_pair:n_pair + n_date]

    date_idx = lax.broadcasted_iota(jnp.int32, (n_pair, n_date), 1)
    sel_a = (pairs_v[:, 0:1] == date_idx).astype(jnp.bfloat16)
    sel_b = (pairs_v[:, 1:2] == date_idx).astype(jnp.bfloat16)
    picked = dot3(split3(looked_pow), jnp.concatenate([sel_a, sel_b], axis=0), False)
    looked_ref = picked[0:n_pair]
    looked_sec = picked[n_pair:2 * n_pair]

    proxy = looked_cross / jnp.sqrt(looked_ref * looked_sec + 1e-06)
    series = dot3(split3(proxy), inv_ref[...], False)
    for s in range(series.shape[0]):
        out_ref[s] = series[s:s + 1, :]


def regroup_kernel(in_hbm, out_ref, in_ref, sems):
    n_chunk = out_ref.shape[0]
    half = n_chunk // 2
    rows_half = half * LOOK_R
    copies = []
    for k in range(2):
        for q in range(2):
            rows = pl.ds(q * rows_half, rows_half)
            copy = pltpu.make_async_copy(in_hbm.at[k, rows], in_ref.at[k, rows], sems.at[2 * k + q])
            copy.start()
            copies.append(copy)
    for k in range(2):
        for q in range(2):
            copies[2 * k + q].wait()
            for c in range(q * half, (q + 1) * half):
                out_ref[c, k * LOOK_R:(k + 1) * LOOK_R, :] = in_ref[k, c * LOOK_R:(c + 1) * LOOK_R, :]


def per_device(slc, pairs, inverse):
    n_date = lax.axis_size("date")
    n_pair = pairs.shape[0]
    steps = inverse.shape[0]
    _, _, all_rows, cols = slc.shape
    rows = all_rows // n_date
    chunks = pl.pallas_call(
        regroup_kernel,
        out_shape=jax.ShapeDtypeStruct((n_date, 2 * rows, cols), slc.dtype),
        in_specs=[pl.BlockSpec(memory_space=pl.ANY)],
        out_specs=pl.BlockSpec(memory_space=pltpu.VMEM),
        scratch_shapes=[pltpu.VMEM(slc.shape[1:], slc.dtype), pltpu.SemaphoreType.DMA((4,))],
    )(slc[0])
    stripes = lax.all_to_all(chunks, "date", split_axis=0, concat_axis=0, tiled=True)
    assert rows == LOOK_R and n_date % 8 == 0 and n_pair % 8 == 0
    looks = cols // LOOK_C
    col = lax.broadcasted_iota(jnp.int32, (cols, looks), 0) // LOOK_C
    window = (col == lax.broadcasted_iota(jnp.int32, (cols, looks), 1)).astype(jnp.bfloat16)
    out = pl.pallas_call(
        functools.partial(kernel, n_date, n_pair),
        out_shape=jax.ShapeDtypeStruct((steps, 1, looks), jnp.float32),
        in_specs=[
            pl.BlockSpec(memory_space=pl.ANY),
            pl.BlockSpec(memory_space=pltpu.VMEM),
            pl.BlockSpec(memory_space=pltpu.VMEM),
            pl.BlockSpec(memory_space=pltpu.VMEM),
            pl.BlockSpec(memory_space=pltpu.VMEM),
        ],
        out_specs=pl.BlockSpec(memory_space=pltpu.VMEM),
        scratch_shapes=[
            pltpu.VMEM((n_date, 2 * LOOK_R, cols), jnp.float32),
            pltpu.VMEM((n_date, 2 * LOOK_R, cols), jnp.float32),
            pltpu.VMEM((n_pair + n_date, cols), jnp.float32),
            pltpu.SMEM(pairs.shape, pairs.dtype),
            pltpu.SemaphoreType.DMA(()),
        ],
        compiler_params=pltpu.CompilerParams(
            vmem_limit_bytes=24 * 1024 * 1024
        ),
    )(pairs, pairs, stripes, inverse, window)
    return out


def solution(mesh):
    in_specs = (P("date", None, "grp", None), P(), P())
    out_specs = P(None, ("grp", "date"), None)
    return jax.shard_map(
        per_device, mesh=mesh, in_specs=in_specs, out_specs=out_specs, check_vma=False
    )
```
